128 devices in a mesh: pages: 32 (over y, x, core), mp: 4 (over z).
Axes of the slice: x: 4, y: 4, z: 4, core: 2. Of those that a mesh axis runs over, the one named last changes fastest.
Arguments:
- tokens: bfloat16 [4, 64, 3072], P(None, None, 'pages'), may hold values from -4.5 to 4.5
- norm_gains: float32 [2, 3072], P(None, 'pages'), may hold values from 0.1 to 1.9
- w_qkv: bfloat16 [3072, 3, 3072], P('pages', None, 'mp'), may hold values from -0.109375 to 0.109375
- w_out: bfloat16 [3072, 3072], P('pages', 'mp'), may hold values from -0.109375 to 0.109375
- w_gate_up: bfloat16 [2, 3072, 8192], P(None, 'pages', 'mp'), may hold values from -0.109375 to 0.109375
- w_down: bfloat16 [3072, 8192], P('pages', 'mp'), may hold values from -0.0625 to 0.0625
- k_cache: bfloat16 [1024, 64, 3072], P('pages', None, 'mp'), may hold values from -1000 to 1000, as said below
- v_cache: bfloat16 [1024, 64, 3072], P('pages', None, 'mp'), may hold values from -6 to 6
- lengths: int32 [64], replicated, may hold values from 1 to 4096, as said below
- slot_request: int32 [1024], replicated, may hold values from -1 to 63, as said below
- slot_page: int32 [1024], replicated, may hold values from 0 to 63
- move_slot: int32 [32, 31], replicated, may hold values from 0 to 31, as said below
- move_offset: int32 [31], replicated, may hold values from 1 to 31, as said below
Outputs:
- layer_out: bfloat16 [4, 64, 3072], P(None, None, 'pages')
- new_k_cache: bfloat16 [1024, 64, 3072], P('pages', None, 'mp')
- new_v_cache: bfloat16 [1024, 64, 3072], P('pages', None, 'mp')
The draws below stay inside these ranges and needn't reach their ends.
Inputs may be any that keep to these rules, and one draw needn't show every extreme that they name: `lengths`: every request holds ceil(length / 64) pages, numbered from 0, each in exactly one slot; the longest holds 4096 tokens. `slot_request`: slots of requests and empty slots lie on holders in no fixed order. `move_slot`: each holder's row names 31 distinct local slots. `move_offset`: every offset from 1 to 31 appears exactly once. `k_cache`: cached keys lie within the range given in the table.
All inputs are finite; a program needn't handle non-finite values.
Results may differ from the reference program's by a relative error of at most 0.018.
The reference program's roundings to bfloat16 on the way count: a program that leaves them out, or rounds other values in their place, can miss the bound.
Values may be sent and summed in bfloat16 or wider, within the bound.
No kernel may reach another device: no remote copies, remote signals or barrier semaphores. Data moves between devices by JAX's collectives and lax.ppermute only.
A program may use at most 128 MiB of HBM per device.

```python
import jax
import jax.numpy as jnp
from jax import lax

D = 3072
HEADS = 32
HEAD_DIM = 96
FF = 8192
REQS = 64
STEPS = 4
PAGE = 64
MAX_PAGES = 64
MOVES = 31
SLOTS = 32
TOTAL_SLOTS = 1024
N_PAGES = 32


def page_layout(key):
    seeded = jax.random.fold_in(key, 101)
    streams = jax.random.split(seeded, 5)
    ranked = jax.random.permutation(streams[0], REQS).astype(jnp.int32)
    rank_ids = jnp.arange(REQS, dtype=jnp.int32)
    added_pages = jax.random.randint(streams[1], (REQS,), 0, 8, dtype=jnp.int32)
    by_rank = jnp.clip(MAX_PAGES // (rank_ids + 1) + added_pages, 1, MAX_PAGES)
    by_rank = by_rank.at[0].set(MAX_PAGES)
    counts = jnp.zeros((REQS,), jnp.int32).at[ranked].set(by_rank)
    last_fill = jax.random.randint(streams[2], (REQS,), 1, PAGE + 1, dtype=jnp.int32)
    last_fill = last_fill.at[ranked[0]].set(PAGE)
    lengths = (counts - 1) * PAGE + last_fill
    listing = jax.random.permutation(streams[3], REQS).astype(jnp.int32)
    listed = counts[listing]
    finish = jnp.cumsum(listed).astype(jnp.int32)
    begins = finish - listed
    places = jnp.arange(TOTAL_SLOTS, dtype=jnp.int32)
    inside = (places[:, None] >= begins[None, :]) & (places[:, None] < finish[None, :])
    entries = jnp.sum(jnp.where(inside, rank_ids[None, :], 0), axis=1)
    filled = jnp.any(inside, axis=1)
    request_at = jnp.where(filled, listing[entries], -1)
    number_at = jnp.where(filled, places - begins[entries], 0)
    speeds = jax.random.randint(streams[4], (N_PAGES,), 1, 5, dtype=jnp.int32)
    priority = places % SLOTS * speeds[places // SLOTS] * TOTAL_SLOTS + places
    ranking = jnp.argsort(priority, stable=True).astype(jnp.int32)
    slot_owner = jnp.full((TOTAL_SLOTS,), -1, jnp.int32).at[ranking].set(request_at)
    slot_number = jnp.zeros((TOTAL_SLOTS,), jnp.int32).at[ranking].set(number_at)
    return (lengths, slot_owner, slot_number)


def draw_lengths(key, part):
    return page_layout(key)[0]


def draw_slot_request(key, part):
    return page_layout(key)[1]


def draw_slot_page(key, part):
    return page_layout(key)[2]


def draw_tokens(key, part):
    streams = jax.random.split(jax.random.fold_in(key, 201), 2)
    columns = jnp.arange(D, dtype=jnp.float32) / D
    column_scale = jnp.exp(jnp.log(3.0) * (columns - 0.5))
    row_scale = jnp.exp(jax.random.uniform(streams[0], (STEPS, REQS, 1), jnp.float32, jnp.log(0.5), jnp.log(2.0)))
    values = jnp.clip(jax.random.normal(streams[1], (STEPS, REQS, D), jnp.float32), -5.0, 5.0)
    return (0.25 * values * row_scale * column_scale).astype(jnp.bfloat16)


def draw_k_cache(key, part):
    streams = jax.random.split(jax.random.fold_in(key, 301), 1)
    values = jnp.clip(jax.random.normal(streams[0], (TOTAL_SLOTS, PAGE, D), jnp.float32), -6.0, 6.0)
    return values.astype(jnp.bfloat16)


def draw_move_slot(key, part):
    streams = jax.random.split(jax.random.fold_in(key, 401), N_PAGES)
    shuffled = jax.vmap(lambda stream: jax.random.permutation(stream, SLOTS))(streams)
    return shuffled[:, :MOVES].astype(jnp.int32)


def draw_move_offset(key, part):
    shuffled = jax.random.permutation(jax.random.fold_in(key, 501), N_PAGES - 1)
    return (shuffled[:MOVES] + 1).astype(jnp.int32)


def level_of(own_key, dims, cuts, smallest, top_value):
    gain = 1.0
    for axis_at, shards_of in cuts:
        steps = jax.random.uniform(jax.random.fold_in(jax.random.fold_in(own_key, 6), axis_at), (shards_of,), jnp.float32, smallest / len(cuts), top_value / len(cuts))
        gain = gain * jnp.repeat(jnp.exp(steps), dims[axis_at] // shards_of).reshape((-1,) + (1,) * (len(dims) - 1 - axis_at))
    return gain


def noise(rng, shape, scale, bound, cuts=(), kind=jnp.bfloat16):
    array = scale * jax.random.normal(rng, shape, jnp.float32)
    if cuts:
        array = array * level_of(rng, shape, cuts, -0.22, 0.18)
    return jnp.clip(array, -bound, bound).astype(kind)


def setup_inputs(seed: int = 0) -> dict:
    streams_of = jax.random.split(jax.random.key(seed), 14)
    return {
        "tokens": draw_tokens(jax.random.fold_in(streams_of[13], 71), 0),
        "norm_gains": jnp.clip(1.0 + 0.18 * jax.random.normal(streams_of[1], (2, D), jnp.float32), 0.1, 1.9),
        "w_qkv": noise(streams_of[2], (D, 3, D), D ** -0.5, 0.109375, ((0, 32), (2, 4))),
        "w_out": noise(streams_of[3], (D, D), D ** -0.5, 0.109375, ((0, 32), (1, 4))),
        "w_gate_up": noise(streams_of[4], (2, D, FF), D ** -0.5, 0.109375, ((1, 32), (2, 4))),
        "w_down": noise(streams_of[5], (D, FF), FF ** -0.5, 0.0625, ((0, 32), (1, 4))),
        "k_cache": draw_k_cache(jax.random.fold_in(streams_of[13], 71), 0),
        "v_cache": noise(streams_of[7], (TOTAL_SLOTS, PAGE, D), 1.0, 6.0, ((0, 32), (2, 4))),
        "lengths": draw_lengths(jax.random.fold_in(streams_of[13], 71), 0),
        "slot_request": draw_slot_request(jax.random.fold_in(streams_of[13], 71), 0),
        "slot_page": draw_slot_page(jax.random.fold_in(streams_of[13], 71), 0),
        "move_slot": draw_move_slot(jax.random.fold_in(streams_of[13], 71), 0),
        "move_offset": draw_move_offset(jax.random.fold_in(streams_of[13], 71), 0),
    }


EPSILON = 1e-05
NEGATIVE = -1e+30
THETA = 10000.0

def rotate(values, positions):
    half_dim = values.shape[-1] // 2
    exponent = jnp.arange(half_dim, dtype=jnp.float32) * (-2.0 / values.shape[-1])
    frequency = jnp.power(jnp.float32(THETA), exponent)
    angles = positions.astype(jnp.float32)[:, None, None] * frequency[None, None, :]
    cosine = jnp.cos(angles)
    sine = jnp.sin(angles)
    first = values[..., :half_dim]
    second = values[..., half_dim:]
    return jnp.concatenate([first * cosine - second * sine, second * cosine + first * sine], axis=-1)

def rounded(values):
    narrow = lax.optimization_barrier(values.astype(jnp.bfloat16))
    return narrow.astype(jnp.float32)

def cached_attention(query, key_new, value_new, k_cache, v_cache, lengths, slot_request, slot_page):
    owners = jnp.clip(slot_request, 0, REQS - 1)
    offsets = jnp.arange(PAGE, dtype=jnp.int32)
    key_pos = slot_page[:, None] * PAGE + offsets[None, :]
    usable = (slot_request >= 0)[:, None] & (key_pos < lengths[owners][:, None])
    request_ids = jnp.arange(REQS, dtype=jnp.int32)
    belongs = slot_request[None, :] == request_ids[:, None]
    indicator = belongs.astype(jnp.float32)
    step_ids = jnp.arange(STEPS, dtype=jnp.int32)
    causal = step_ids[:, None] >= step_ids[None, :]
    scale = HEAD_DIM ** (-0.5)

    def one_head(head):

        def pick(table):
            return lax.dynamic_slice_in_dim(table, head * HEAD_DIM, HEAD_DIM, 1).reshape(STEPS, REQS, HEAD_DIM).astype(jnp.float32)
        query_head = pick(query)
        key_head = pick(key_new)
        value_head = pick(value_new)
        cache_keys = lax.dynamic_slice_in_dim(k_cache, head * HEAD_DIM, HEAD_DIM, 2).astype(jnp.float32)
        cache_vals = lax.dynamic_slice_in_dim(v_cache, head * HEAD_DIM, HEAD_DIM, 2).astype(jnp.float32)
        per_slot = query_head[:, owners]
        cached = jnp.einsum('tsd,skd->tsk', per_slot, cache_keys) * scale
        cached = jnp.where(usable[None], cached, NEGATIVE)
        fresh = jnp.einsum('trd,urd->tur', query_head, key_head) * scale
        fresh = jnp.where(causal[:, :, None], fresh, NEGATIVE)
        slot_top = lax.optimization_barrier(jnp.max(cached, axis=2))
        cache_top = lax.optimization_barrier(jnp.max(jnp.where(belongs[None], slot_top[:, None, :], NEGATIVE), axis=2))
        row_top = jnp.maximum(cache_top, lax.optimization_barrier(jnp.max(fresh, axis=1)))
        cached_w = jnp.where(usable[None], jnp.exp(cached - row_top[:, owners][:, :, None]), 0.0)
        fresh_w = jnp.where(causal[:, :, None], jnp.exp(fresh - row_top[:, None, :]), 0.0)
        totals = jnp.einsum('rs,ts->tr', indicator, lax.optimization_barrier(jnp.sum(cached_w, axis=2)), precision=lax.Precision.HIGHEST) + lax.optimization_barrier(jnp.sum(fresh_w, axis=1))
        slot_acc = jnp.einsum('tsk,skd->tsd', rounded(cached_w), cache_vals)
        summed = jnp.einsum('rs,tsd->trd', indicator, slot_acc, precision=lax.Precision.HIGHEST)
        summed = summed + jnp.einsum('tur,urd->trd', rounded(fresh_w), value_head)
        return (summed / totals[:, :, None]).astype(jnp.bfloat16)
    stacked = lax.map(one_head, jnp.arange(HEADS, dtype=jnp.int32))
    return stacked.transpose(1, 2, 0, 3).reshape(STEPS * REQS, D)

def migrate(pool, move_slot, move_offset):
    holder_ids = jnp.arange(N_PAGES, dtype=jnp.int32)[:, None]
    move_ids = jnp.arange(MOVES, dtype=jnp.int32)[None, :]
    source_holder = (holder_ids - move_offset[None, :]) % N_PAGES
    destination = holder_ids * SLOTS + move_slot
    anchor = source_holder * SLOTS + move_slot[source_holder, move_ids]
    mapping = jnp.arange(TOTAL_SLOTS, dtype=jnp.int32).at[destination.reshape(-1)].set(anchor.reshape(-1))
    return pool[mapping]

def reference(tokens, norm_gains, w_qkv, w_out, w_gate_up, w_down, k_cache, v_cache, lengths, slot_request, slot_page, move_slot, move_offset):
    row_count = STEPS * REQS
    activ = tokens.reshape(row_count, D).astype(jnp.float32)
    row_ids = jnp.arange(row_count, dtype=jnp.int32)
    positions = lengths[row_ids % REQS] + row_ids // REQS
    inverse_one = lax.rsqrt(lax.optimization_barrier(jnp.sum(activ * activ, axis=1)) / D + EPSILON)
    normed_one = (activ * norm_gains[0]).astype(jnp.bfloat16)
    projected = jnp.dot(normed_one, w_qkv.reshape(D, 3 * D), preferred_element_type=jnp.float32) * inverse_one[:, None]
    projected = projected.reshape(row_count, 3, HEADS, HEAD_DIM)
    query = rotate(projected[:, 0], positions).astype(jnp.bfloat16).reshape(row_count, D)
    key_new = rotate(projected[:, 1], positions).astype(jnp.bfloat16).reshape(row_count, D)
    value_new = projected[:, 2].astype(jnp.bfloat16).reshape(row_count, D)
    attended = cached_attention(query, key_new, value_new, k_cache, v_cache, lengths, slot_request, slot_page)
    mixed = activ + jnp.dot(attended, w_out.T, preferred_element_type=jnp.float32)
    inverse_two = lax.rsqrt(lax.optimization_barrier(jnp.sum(mixed * mixed, axis=1)) / D + EPSILON)
    normed_two = (mixed * norm_gains[1]).astype(jnp.bfloat16)
    gate = jnp.dot(normed_two, w_gate_up[0], preferred_element_type=jnp.float32) * inverse_two[:, None]
    upward = jnp.dot(normed_two, w_gate_up[1], preferred_element_type=jnp.float32) * inverse_two[:, None]
    hidden = (jax.nn.silu(gate) * upward).astype(jnp.bfloat16)
    layer_out = (mixed + jnp.dot(hidden, w_down.T, preferred_element_type=jnp.float32)).astype(jnp.bfloat16)
    new_k_cache = migrate(k_cache, move_slot, move_offset)
    new_v_cache = migrate(v_cache, move_slot, move_offset)
    return (layer_out.reshape(STEPS, REQS, D), new_k_cache, new_v_cache)
```

```python
import jax
import jax.numpy as jnp
from jax import lax
from jax.sharding import PartitionSpec as P

D = 3072
HEAD_DIM = 96


EPSILON = 1e-05
NEGATIVE = -1e30
THETA = 10000.0
CONTRACT_LAST = (((1,), (1,)), ((), ()))


def merged(part, axis, combine):
    gathered = jax.tree.map(lambda a: lax.all_gather(a, axis), part)

    def take(source):
        return jax.tree.map(lambda a: lax.dynamic_index_in_dim(a, source, 0, False), gathered)

    return lax.fori_loop(
        1, lax.axis_size(axis), lambda source, state: combine(state, take(source)), take(0)
    )


def rotate(values, positions):
    half_dim = values.shape[-1] // 2
    exponent = jnp.arange(half_dim, dtype=jnp.float32) * (-2.0 / values.shape[-1])
    frequency = jnp.power(jnp.float32(THETA), exponent)
    angles = positions.astype(jnp.float32)[:, None, None] * frequency[None, None, :]
    cosine = jnp.cos(angles)
    sine = jnp.sin(angles)
    first = values[..., :half_dim]
    second = values[..., half_dim:]
    return jnp.concatenate(
        [first * cosine - second * sine, second * cosine + first * sine], axis=-1
    )


def merge_parts(first, second):
    top_a, total_a, accum_a = first
    top_b, total_b, accum_b = second
    joined = jnp.maximum(top_a, top_b)
    factor_a = jnp.exp(top_a - joined)
    factor_b = jnp.exp(top_b - joined)
    return (
        joined,
        total_a * factor_a + total_b * factor_b,
        accum_a * factor_a[..., None] + accum_b * factor_b[..., None],
    )


def reduce_rows(partial_value, squares, finish):
    rows = partial_value.shape[0]
    packed = jnp.concatenate([partial_value.reshape(rows, -1), squares[:, None]], axis=1)
    packed = lax.psum(packed, "pages")
    total = packed[:, :-1].reshape(partial_value.shape)
    return finish(total, packed[:, -1], 0)


def across_heads(term):
    return lax.psum(term, "mp")


def migrate_pool(key_local, value_local, move_slot, move_offset):
    holders = lax.axis_size("pages")
    myself = lax.axis_index("pages")
    mine = lax.dynamic_index_in_dim(move_slot, myself, 0, keepdims=False)
    targets = (myself + move_offset) % holders
    holder_ids = jnp.arange(holders, dtype=jnp.int32)
    aimed = holder_ids[:, None] == targets[None, :]
    chosen = jnp.sum(jnp.where(aimed, mine[None, :], 0), axis=1)
    sending = jnp.any(aimed, axis=1)[:, None, None]
    key_send = jnp.where(sending, key_local[chosen], jnp.zeros((), key_local.dtype))
    value_send = jnp.where(sending, value_local[chosen], jnp.zeros((), value_local.dtype))
    key_recv, value_recv = (
        lax.all_to_all(key_send, "pages", split_axis=0, concat_axis=0, tiled=True),
        lax.all_to_all(value_send, "pages", split_axis=0, concat_axis=0, tiled=True),
    )
    sources = (myself - move_offset) % holders
    slot_ids = jnp.arange(key_local.shape[0], dtype=jnp.int32)
    landing = slot_ids[:, None] == mine[None, :]
    came_from = jnp.sum(jnp.where(landing, sources[None, :], 0), axis=1)
    arriving = jnp.any(landing, axis=1)[:, None, None]
    return (
        jnp.where(arriving, key_recv[came_from], key_local),
        jnp.where(arriving, value_recv[came_from], value_local),
    )


def local_attention(queries, k_cache, v_cache, lengths, slot_request, slot_page):
    step_count, req_count, heads_here, head_dim = queries.shape
    slot_count, page_len, channels = k_cache.shape
    scale = head_dim ** (-0.5)
    myself = lax.axis_index("pages")
    own_request = lax.dynamic_slice_in_dim(slot_request, myself * slot_count, slot_count)
    own_page = lax.dynamic_slice_in_dim(slot_page, myself * slot_count, slot_count)
    owners = jnp.clip(own_request, 0, req_count - 1)
    key_pos = own_page[:, None] * page_len + jnp.arange(page_len, dtype=jnp.int32)[None, :]
    usable = (own_request >= 0)[:, None] & (key_pos < lengths[owners][:, None])
    keys_here = k_cache.reshape(slot_count, page_len, heads_here, head_dim)
    values_here = v_cache.reshape(slot_count, page_len, heads_here, head_dim)
    scores = (
        jnp.einsum(
            "tshd,skhd->tshk", queries[:, owners], keys_here, preferred_element_type=jnp.float32
        )
        * scale
    )
    live_mask = usable[None, :, None, :]
    scores = jnp.where(live_mask, scores, NEGATIVE)
    slot_top = jnp.max(scores, axis=3)
    belongs = own_request[None, :] == jnp.arange(req_count, dtype=jnp.int32)[:, None]
    request_top = jnp.max(
        jnp.where(belongs[None, :, :, None], slot_top[:, None, :, :], NEGATIVE), axis=2
    )
    weights = jnp.where(live_mask, jnp.exp(scores - request_top[:, owners][..., None]), 0.0)
    slot_total = jnp.sum(weights, axis=3)
    slot_acc = jnp.einsum(
        "tshk,skhd->tshd",
        weights.astype(jnp.bfloat16),
        values_here,
        preferred_element_type=jnp.float32,
    )
    indicator = belongs.astype(jnp.float32)
    totals = jnp.einsum("rs,tsh->trh", indicator, slot_total, precision=lax.Precision.HIGHEST)
    accums = jnp.einsum("rs,tshd->trhd", indicator, slot_acc, precision=lax.Precision.HIGHEST)
    return (request_top, totals, accums)


def shards(
    tokens,
    norm_gains,
    w_qkv,
    w_out,
    w_gate_up,
    w_down,
    k_cache,
    v_cache,
    lengths,
    slot_request,
    slot_page,
    move_slot,
    move_offset,
):
    step_count, req_count, width_here = tokens.shape
    row_count = step_count * req_count
    activ = tokens.reshape(row_count, width_here).astype(jnp.float32)
    row_ids = jnp.arange(row_count, dtype=jnp.int32)
    positions = lengths[row_ids % req_count] + row_ids // req_count

    def finish_qkv(total, squares, start):
        count = total.shape[0]
        inverse = lax.rsqrt(squares / D + EPSILON)
        scaled = total * inverse[:, None, None]
        heads_here = scaled.shape[2] // HEAD_DIM
        query_rows = rotate(scaled[:, 0].reshape(count, heads_here, HEAD_DIM), positions)
        key_rows = rotate(scaled[:, 1].reshape(count, heads_here, HEAD_DIM), positions)
        return (
            query_rows.reshape(count, -1).astype(jnp.bfloat16),
            key_rows.reshape(count, -1).astype(jnp.bfloat16),
            scaled[:, 2].astype(jnp.bfloat16),
        )

    def finish_mlp(total, squares, start):
        inverse = lax.rsqrt(squares / D + EPSILON)
        gate = total[:, 0] * inverse[:, None]
        upward = total[:, 1] * inverse[:, None]
        return ((jax.nn.silu(gate) * upward).astype(jnp.bfloat16),)

    normed_one = (activ * norm_gains[0]).astype(jnp.bfloat16)
    partial_one = jnp.einsum("bd,dcn->bcn", normed_one, w_qkv, preferred_element_type=jnp.float32)
    squares_one = jnp.sum(activ * activ, axis=1)
    query_all, key_all, value_all = reduce_rows(partial_one, squares_one, finish_qkv)
    heads_here = query_all.shape[1] // HEAD_DIM
    queries = query_all.reshape(step_count, req_count, heads_here, HEAD_DIM)
    key_fresh = key_all.reshape(step_count, req_count, heads_here, HEAD_DIM)
    value_fresh = value_all.reshape(step_count, req_count, heads_here, HEAD_DIM)
    cache_top, cache_total, cache_acc = local_attention(
        queries, k_cache, v_cache, lengths, slot_request, slot_page
    )
    holders = lax.axis_size("pages")
    myself = lax.axis_index("pages")
    group = req_count // holders
    packed = jnp.concatenate(
        [cache_acc, cache_total[..., None], cache_top[..., None]], axis=-1
    ).reshape(step_count, holders, group, heads_here, HEAD_DIM + 2)
    packed = jnp.moveaxis(packed, 1, 0)
    packed = lax.all_to_all(packed, "pages", split_axis=0, concat_axis=0, tiled=True)
    part_acc = packed[..., :HEAD_DIM]
    part_total = packed[..., HEAD_DIM]
    part_top = packed[..., HEAD_DIM + 1]
    mine = lambda a: lax.dynamic_slice_in_dim(a, myself * group, group, 1)
    queries_mine = mine(queries)
    key_mine = mine(key_fresh)
    value_mine = mine(value_fresh)
    scale = HEAD_DIM ** (-0.5)
    step_ids = jnp.arange(step_count, dtype=jnp.int32)
    causal = (step_ids[:, None] >= step_ids[None, :])[:, :, None, None]
    fresh = (
        jnp.einsum("trhd,urhd->turh", queries_mine, key_mine, preferred_element_type=jnp.float32)
        * scale
    )
    fresh = jnp.where(causal, fresh, NEGATIVE)
    row_top = jnp.maximum(jnp.max(part_top, axis=0), jnp.max(fresh, axis=1))
    carried = jnp.exp(part_top - row_top[None])
    fresh_w = jnp.where(causal, jnp.exp(fresh - row_top[:, None]), 0.0)
    totals = jnp.sum(part_total * carried, axis=0) + jnp.sum(fresh_w, axis=1)
    accums = jnp.sum(part_acc * carried[..., None], axis=0) + jnp.einsum(
        "turh,urhd->trhd",
        fresh_w.astype(jnp.bfloat16),
        value_mine,
        preferred_element_type=jnp.float32,
    )
    attended_mine = (accums / totals[..., None]).astype(jnp.bfloat16)
    attended = lax.all_gather(attended_mine, "pages", axis=1, tiled=True).reshape(
        row_count, heads_here * HEAD_DIM
    )
    mixed = activ + across_heads(
        lax.dot_general(attended, w_out, CONTRACT_LAST, preferred_element_type=jnp.float32)
    )
    normed_two = (mixed * norm_gains[1]).astype(jnp.bfloat16)
    partial_two = jnp.einsum(
        "bd,gdf->bgf", normed_two, w_gate_up, preferred_element_type=jnp.float32
    )
    squares_two = jnp.sum(mixed * mixed, axis=1)
    (hidden,) = reduce_rows(partial_two, squares_two, finish_mlp)
    feed = across_heads(
        lax.dot_general(hidden, w_down, CONTRACT_LAST, preferred_element_type=jnp.float32)
    )
    layer_out = (mixed + feed).astype(jnp.bfloat16).reshape(step_count, req_count, width_here)
    new_k_cache, new_v_cache = migrate_pool(k_cache, v_cache, move_slot, move_offset)
    return (layer_out, new_k_cache, new_v_cache)


def solution(mesh):
    in_specs = (
        P(None, None, "pages"),
        P(None, "pages"),
        P("pages", None, "mp"),
        P("pages", "mp"),
        P(None, "pages", "mp"),
        P("pages", "mp"),
        P("pages", None, "mp"),
        P("pages", None, "mp"),
        P(),
        P(),
        P(),
        P(),
        P(),
    )
    out_specs = (P(None, None, "pages"), P("pages", None, "mp"), P("pages", None, "mp"))
    return jax.shard_map(shards, mesh=mesh, in_specs=in_specs, out_specs=out_specs, check_vma=False)
```

```python
import jax
import jax.numpy as jnp
from jax import lax
from jax.sharding import PartitionSpec as P

D = 3072
HEAD_DIM = 96


EPSILON = 1e-05
NEGATIVE = -1e30
THETA = 10000.0
CONTRACT_LAST = (((1,), (1,)), ((), ()))


def merged(part, axis, combine):
    gathered = jax.tree.map(lambda a: lax.all_gather(a, axis), part)

    def take(source):
        return jax.tree.map(lambda a: lax.dynamic_index_in_dim(a, source, 0, False), gathered)

    return lax.fori_loop(
        1, lax.axis_size(axis), lambda source, state: combine(state, take(source)), take(0)
    )


def rotate(values, positions):
    half_dim = values.shape[-1] // 2
    exponent = jnp.arange(half_dim, dtype=jnp.float32) * (-2.0 / values.shape[-1])
    frequency = jnp.power(jnp.float32(THETA), exponent)
    angles = positions.astype(jnp.float32)[:, None, None] * frequency[None, None, :]
    cosine = jnp.cos(angles)
    sine = jnp.sin(angles)
    first = values[..., :half_dim]
    second = values[..., half_dim:]
    return jnp.concatenate(
        [first * cosine - second * sine, second * cosine + first * sine], axis=-1
    )


def merge_parts(first, second):
    top_a, total_a, accum_a = first
    top_b, total_b, accum_b = second
    joined = jnp.maximum(top_a, top_b)
    factor_a = jnp.exp(top_a - joined)
    factor_b = jnp.exp(top_b - joined)
    return (
        joined,
        total_a * factor_a + total_b * factor_b,
        accum_a * factor_a[..., None] + accum_b * factor_b[..., None],
    )


def reduce_rows(partial_value, squares, finish):
    rows = partial_value.shape[0]
    packed = jnp.concatenate([partial_value.reshape(rows, -1), squares[:, None]], axis=1)
    packed = lax.psum(packed, "pages")
    total = packed[:, :-1].reshape(partial_value.shape)
    return finish(total, packed[:, -1], 0)


def gather_blocks(block, axis):
    count = lax.axis_size(axis)
    spread = jnp.broadcast_to(block[None], (count,) + block.shape)
    return lax.all_to_all(spread, axis, split_axis=0, concat_axis=0, tiled=True)


def across_heads(term):
    return jnp.sum(gather_blocks(term, "mp"), axis=0)


def migrate_pool(key_local, value_local, move_slot, move_offset):
    holders = lax.axis_size("pages")
    myself = lax.axis_index("pages")
    mine = lax.dynamic_index_in_dim(move_slot, myself, 0, keepdims=False)
    targets = (myself + move_offset) % holders
    holder_ids = jnp.arange(holders, dtype=jnp.int32)
    aimed = holder_ids[:, None] == targets[None, :]
    chosen = jnp.sum(jnp.where(aimed, mine[None, :], 0), axis=1)
    sending = jnp.any(aimed, axis=1)[:, None, None]
    key_send = jnp.where(sending, key_local[chosen], jnp.zeros((), key_local.dtype))
    value_send = jnp.where(sending, value_local[chosen], jnp.zeros((), value_local.dtype))
    key_recv, value_recv = (
        lax.all_to_all(key_send, "pages", split_axis=0, concat_axis=0, tiled=True),
        lax.all_to_all(value_send, "pages", split_axis=0, concat_axis=0, tiled=True),
    )
    sources = (myself - move_offset) % holders
    slot_ids = jnp.arange(key_local.shape[0], dtype=jnp.int32)
    landing = slot_ids[:, None] == mine[None, :]
    came_from = jnp.sum(jnp.where(landing, sources[None, :], 0), axis=1)
    arriving = jnp.any(landing, axis=1)[:, None, None]
    return (
        jnp.where(arriving, key_recv[came_from], key_local),
        jnp.where(arriving, value_recv[came_from], value_local),
    )


def local_attention(queries, k_cache, v_cache, lengths, slot_request, slot_page):
    step_count, req_count, heads_here, head_dim = queries.shape
    slot_count, page_len, channels = k_cache.shape
    scale = head_dim ** (-0.5)
    myself = lax.axis_index("pages")
    own_request = lax.dynamic_slice_in_dim(slot_request, myself * slot_count, slot_count)
    own_page = lax.dynamic_slice_in_dim(slot_page, myself * slot_count, slot_count)
    owners = jnp.clip(own_request, 0, req_count - 1)
    key_pos = own_page[:, None] * page_len + jnp.arange(page_len, dtype=jnp.int32)[None, :]
    usable = (own_request >= 0)[:, None] & (key_pos < lengths[owners][:, None])
    keys_here = k_cache.reshape(slot_count, page_len, heads_here, head_dim)
    values_here = v_cache.reshape(slot_count, page_len, heads_here, head_dim)
    scores = (
        jnp.einsum(
            "tshd,skhd->tshk", queries[:, owners], keys_here, preferred_element_type=jnp.float32
        )
        * scale
    )
    live_mask = usable[None, :, None, :]
    scores = jnp.where(live_mask, scores, NEGATIVE)
    slot_top = jnp.max(scores, axis=3)
    belongs = own_request[None, :] == jnp.arange(req_count, dtype=jnp.int32)[:, None]
    request_top = jnp.max(
        jnp.where(belongs[None, :, :, None], slot_top[:, None, :, :], NEGATIVE), axis=2
    )
    weights = jnp.where(live_mask, jnp.exp(scores - request_top[:, owners][..., None]), 0.0)
    slot_total = jnp.sum(weights, axis=3)
    slot_acc = jnp.einsum(
        "tshk,skhd->tshd",
        weights.astype(jnp.bfloat16),
        values_here,
        preferred_element_type=jnp.float32,
    )
    indicator = belongs.astype(jnp.float32)
    totals = jnp.einsum("rs,tsh->trh", indicator, slot_total, precision=lax.Precision.HIGHEST)
    accums = jnp.einsum("rs,tshd->trhd", indicator, slot_acc, precision=lax.Precision.HIGHEST)
    return (request_top, totals, accums)


def shards(
    tokens,
    norm_gains,
    w_qkv,
    w_out,
    w_gate_up,
    w_down,
    k_cache,
    v_cache,
    lengths,
    slot_request,
    slot_page,
    move_slot,
    move_offset,
):
    step_count, req_count, width_here = tokens.shape
    row_count = step_count * req_count
    activ = tokens.reshape(row_count, width_here).astype(jnp.float32)
    row_ids = jnp.arange(row_count, dtype=jnp.int32)
    positions = lengths[row_ids % req_count] + row_ids // req_count

    def finish_qkv(total, squares, start):
        count = total.shape[0]
        inverse = lax.rsqrt(squares / D + EPSILON)
        scaled = total * inverse[:, None, None]
        heads_here = scaled.shape[2] // HEAD_DIM
        query_rows = rotate(scaled[:, 0].reshape(count, heads_here, HEAD_DIM), positions)
        key_rows = rotate(scaled[:, 1].reshape(count, heads_here, HEAD_DIM), positions)
        return (
            query_rows.reshape(count, -1).astype(jnp.bfloat16),
            key_rows.reshape(count, -1).astype(jnp.bfloat16),
            scaled[:, 2].astype(jnp.bfloat16),
        )

    def finish_mlp(total, squares, start):
        inverse = lax.rsqrt(squares / D + EPSILON)
        gate = total[:, 0] * inverse[:, None]
        upward = total[:, 1] * inverse[:, None]
        return ((jax.nn.silu(gate) * upward).astype(jnp.bfloat16),)

    normed_one = (activ * norm_gains[0]).astype(jnp.bfloat16)
    partial_one = jnp.einsum("bd,dcn->bcn", normed_one, w_qkv, preferred_element_type=jnp.float32)
    squares_one = jnp.sum(activ * activ, axis=1)
    query_all, key_all, value_all = reduce_rows(partial_one, squares_one, finish_qkv)
    heads_here = query_all.shape[1] // HEAD_DIM
    queries = query_all.reshape(step_count, req_count, heads_here, HEAD_DIM)
    key_fresh = key_all.reshape(step_count, req_count, heads_here, HEAD_DIM)
    value_fresh = value_all.reshape(step_count, req_count, heads_here, HEAD_DIM)
    cache_top, cache_total, cache_acc = local_attention(
        queries, k_cache, v_cache, lengths, slot_request, slot_page
    )
    holders = lax.axis_size("pages")
    myself = lax.axis_index("pages")
    group = req_count // holders
    packed = jnp.concatenate(
        [cache_acc, cache_total[..., None], cache_top[..., None]], axis=-1
    ).reshape(step_count, holders, group, heads_here, HEAD_DIM + 2)
    packed = jnp.moveaxis(packed, 1, 0)
    packed = lax.all_to_all(packed, "pages", split_axis=0, concat_axis=0, tiled=True)
    part_acc = packed[..., :HEAD_DIM]
    part_total = packed[..., HEAD_DIM]
    part_top = packed[..., HEAD_DIM + 1]
    mine = lambda a: lax.dynamic_slice_in_dim(a, myself * group, group, 1)
    queries_mine = mine(queries)
    key_mine = mine(key_fresh)
    value_mine = mine(value_fresh)
    scale = HEAD_DIM ** (-0.5)
    step_ids = jnp.arange(step_count, dtype=jnp.int32)
    causal = (step_ids[:, None] >= step_ids[None, :])[:, :, None, None]
    fresh = (
        jnp.einsum("trhd,urhd->turh", queries_mine, key_mine, preferred_element_type=jnp.float32)
        * scale
    )
    fresh = jnp.where(causal, fresh, NEGATIVE)
    row_top = jnp.maximum(jnp.max(part_top, axis=0), jnp.max(fresh, axis=1))
    carried = jnp.exp(part_top - row_top[None])
    fresh_w = jnp.where(causal, jnp.exp(fresh - row_top[:, None]), 0.0)
    totals = jnp.sum(part_total * carried, axis=0) + jnp.sum(fresh_w, axis=1)
    accums = jnp.sum(part_acc * carried[..., None], axis=0) + jnp.einsum(
        "turh,urhd->trhd",
        fresh_w.astype(jnp.bfloat16),
        value_mine,
        preferred_element_type=jnp.float32,
    )
    attended_mine = (accums / totals[..., None]).astype(jnp.bfloat16)
    attended = jnp.moveaxis(gather_blocks(attended_mine, "pages"), 0, 1).reshape(
        row_count, heads_here * HEAD_DIM
    )
    mixed = activ + across_heads(
        lax.dot_general(attended, w_out, CONTRACT_LAST, preferred_element_type=jnp.float32)
    )
    normed_two = (mixed * norm_gains[1]).astype(jnp.bfloat16)
    partial_two = jnp.einsum(
        "bd,gdf->bgf", normed_two, w_gate_up, preferred_element_type=jnp.float32
    )
    squares_two = jnp.sum(mixed * mixed, axis=1)
    (hidden,) = reduce_rows(partial_two, squares_two, finish_mlp)
    feed = across_heads(
        lax.dot_general(hidden, w_down, CONTRACT_LAST, preferred_element_type=jnp.float32)
    )
    layer_out = (mixed + feed).astype(jnp.bfloat16).reshape(step_count, req_count, width_here)
    new_k_cache, new_v_cache = migrate_pool(k_cache, v_cache, move_slot, move_offset)
    return (layer_out, new_k_cache, new_v_cache)


def solution(mesh):
    in_specs = (
        P(None, None, "pages"),
        P(None, "pages"),
        P("pages", None, "mp"),
        P("pages", "mp"),
        P(None, "pages", "mp"),
        P("pages", "mp"),
        P("pages", None, "mp"),
        P("pages", None, "mp"),
        P(),
        P(),
        P(),
        P(),
        P(),
    )
    out_specs = (P(None, None, "pages"), P("pages", None, "mp"), P("pages", None, "mp"))
    return jax.shard_map(shards, mesh=mesh, in_specs=in_specs, out_specs=out_specs, check_vma=False)
```

```python
import jax
import jax.numpy as jnp
from jax import lax
from jax.sharding import PartitionSpec as P

D = 3072
HEAD_DIM = 96


EPSILON = 1e-05
NEGATIVE = -1e30
THETA = 10000.0
CONTRACT_LAST = (((1,), (1,)), ((), ()))


def merged(part, axis, combine):
    gathered = jax.tree.map(lambda a: lax.all_gather(a, axis), part)

    def take(source):
        return jax.tree.map(lambda a: lax.dynamic_index_in_dim(a, source, 0, False), gathered)

    return lax.fori_loop(
        1, lax.axis_size(axis), lambda source, state: combine(state, take(source)), take(0)
    )


def rotate(values, positions):
    half_dim = values.shape[-1] // 2
    exponent = jnp.arange(half_dim, dtype=jnp.float32) * (-2.0 / values.shape[-1])
    frequency = jnp.power(jnp.float32(THETA), exponent)
    angles = positions.astype(jnp.float32)[:, None, None] * frequency[None, None, :]
    cosine = jnp.cos(angles)
    sine = jnp.sin(angles)
    first = values[..., :half_dim]
    second = values[..., half_dim:]
    return jnp.concatenate(
        [first * cosine - second * sine, second * cosine + first * sine], axis=-1
    )


def merge_parts(first, second):
    top_a, total_a, accum_a = first
    top_b, total_b, accum_b = second
    joined = jnp.maximum(top_a, top_b)
    factor_a = jnp.exp(top_a - joined)
    factor_b = jnp.exp(top_b - joined)
    return (
        joined,
        total_a * factor_a + total_b * factor_b,
        accum_a * factor_a[..., None] + accum_b * factor_b[..., None],
    )


def reduce_rows(partial_value, squares, finish, tied=()):
    rows = partial_value.shape[0]
    packed = jnp.concatenate([partial_value.reshape(rows, -1), squares[:, None]], axis=1)
    packed = lax.psum(packed, "pages")
    if tied:
        packed, tied = lax.optimization_barrier((packed, tied))
        return finish(packed[:, :-1].reshape(partial_value.shape), packed[:, -1], 0), tied
    total = packed[:, :-1].reshape(partial_value.shape)
    return finish(total, packed[:, -1], 0)


def gather_blocks(block, axis):
    count = lax.axis_size(axis)
    spread = jnp.broadcast_to(block[None], (count,) + block.shape)
    return lax.all_to_all(spread, axis, split_axis=0, concat_axis=0, tiled=True)


def across_heads(term):
    return jnp.sum(gather_blocks(term, "mp"), axis=0)


def migrate_pool(key_local, value_local, move_slot, move_offset):
    holders = lax.axis_size("pages")
    myself = lax.axis_index("pages")
    mine = lax.dynamic_index_in_dim(move_slot, myself, 0, keepdims=False)
    targets = (myself + move_offset) % holders
    holder_ids = jnp.arange(holders, dtype=jnp.int32)
    aimed = holder_ids[:, None] == targets[None, :]
    chosen = jnp.sum(jnp.where(aimed, mine[None, :], 0), axis=1)
    sending = jnp.any(aimed, axis=1)[:, None, None]
    key_send = jnp.where(sending, key_local[chosen], jnp.zeros((), key_local.dtype))
    value_send = jnp.where(sending, value_local[chosen], jnp.zeros((), value_local.dtype))
    both = lax.all_to_all(
        jnp.stack([key_send, value_send], axis=1), "pages", split_axis=0, concat_axis=0, tiled=True
    )
    return both[:, 0], both[:, 1]


def land_pool(key_local, value_local, key_recv, value_recv, move_slot, move_offset):
    holders = lax.axis_size("pages")
    myself = lax.axis_index("pages")
    mine = lax.dynamic_index_in_dim(move_slot, myself, 0, keepdims=False)
    sources = (myself - move_offset) % holders
    slot_ids = jnp.arange(key_local.shape[0], dtype=jnp.int32)
    landing = slot_ids[:, None] == mine[None, :]
    came_from = jnp.sum(jnp.where(landing, sources[None, :], 0), axis=1)
    arriving = jnp.any(landing, axis=1)[:, None, None]
    return (
        jnp.where(arriving, key_recv[came_from], key_local),
        jnp.where(arriving, value_recv[came_from], value_local),
    )


def local_attention(queries, k_cache, v_cache, lengths, slot_request, slot_page):
    step_count, req_count, heads_here, head_dim = queries.shape
    slot_count, page_len, channels = k_cache.shape
    scale = head_dim ** (-0.5)
    myself = lax.axis_index("pages")
    own_request = lax.dynamic_slice_in_dim(slot_request, myself * slot_count, slot_count)
    own_page = lax.dynamic_slice_in_dim(slot_page, myself * slot_count, slot_count)
    owners = jnp.clip(own_request, 0, req_count - 1)
    key_pos = own_page[:, None] * page_len + jnp.arange(page_len, dtype=jnp.int32)[None, :]
    usable = (own_request >= 0)[:, None] & (key_pos < lengths[owners][:, None])
    keys_here = k_cache.reshape(slot_count, page_len, heads_here, head_dim)
    values_here = v_cache.reshape(slot_count, page_len, heads_here, head_dim)
    scores = (
        jnp.einsum(
            "tshd,skhd->tshk", queries[:, owners], keys_here, preferred_element_type=jnp.float32
        )
        * scale
    )
    live_mask = usable[None, :, None, :]
    scores = jnp.where(live_mask, scores, NEGATIVE)
    slot_top = jnp.max(scores, axis=3)
    belongs = own_request[None, :] == jnp.arange(req_count, dtype=jnp.int32)[:, None]
    request_top = jnp.max(
        jnp.where(belongs[None, :, :, None], slot_top[:, None, :, :], NEGATIVE), axis=2
    )
    weights = jnp.where(live_mask, jnp.exp(scores - request_top[:, owners][..., None]), 0.0)
    slot_total = jnp.sum(weights, axis=3)
    slot_acc = jnp.einsum(
        "tshk,skhd->tshd",
        weights.astype(jnp.bfloat16),
        values_here,
        preferred_element_type=jnp.float32,
    )
    indicator = belongs.astype(jnp.float32)
    totals = jnp.einsum("rs,tsh->trh", indicator, slot_total, precision=lax.Precision.HIGHEST)
    accums = jnp.einsum("rs,tshd->trhd", indicator, slot_acc, precision=lax.Precision.HIGHEST)
    return (request_top, totals, accums)


def shards(
    tokens,
    norm_gains,
    w_qkv,
    w_out,
    w_gate_up,
    w_down,
    k_cache,
    v_cache,
    lengths,
    slot_request,
    slot_page,
    move_slot,
    move_offset,
):
    step_count, req_count, width_here = tokens.shape
    row_count = step_count * req_count
    activ = tokens.reshape(row_count, width_here).astype(jnp.float32)
    row_ids = jnp.arange(row_count, dtype=jnp.int32)
    positions = lengths[row_ids % req_count] + row_ids // req_count

    def finish_qkv(total, squares, start):
        count = total.shape[0]
        inverse = lax.rsqrt(squares / D + EPSILON)
        scaled = total * inverse[:, None, None]
        heads_here = scaled.shape[2] // HEAD_DIM
        query_rows = rotate(scaled[:, 0].reshape(count, heads_here, HEAD_DIM), positions)
        key_rows = rotate(scaled[:, 1].reshape(count, heads_here, HEAD_DIM), positions)
        return (
            query_rows.reshape(count, -1).astype(jnp.bfloat16),
            key_rows.reshape(count, -1).astype(jnp.bfloat16),
            scaled[:, 2].astype(jnp.bfloat16),
        )

    def finish_mlp(total, squares, start):
        inverse = lax.rsqrt(squares / D + EPSILON)
        gate = total[:, 0] * inverse[:, None]
        upward = total[:, 1] * inverse[:, None]
        return ((jax.nn.silu(gate) * upward).astype(jnp.bfloat16),)

    normed_one = (activ * norm_gains[0]).astype(jnp.bfloat16)
    partial_one = jnp.einsum("bd,dcn->bcn", normed_one, w_qkv, preferred_element_type=jnp.float32)
    squares_one = jnp.sum(activ * activ, axis=1)
    received = migrate_pool(k_cache, v_cache, move_slot, move_offset)
    (query_all, key_all, value_all), received = reduce_rows(
        partial_one, squares_one, finish_qkv, received
    )
    heads_here = query_all.shape[1] // HEAD_DIM
    queries = query_all.reshape(step_count, req_count, heads_here, HEAD_DIM)
    key_fresh = key_all.reshape(step_count, req_count, heads_here, HEAD_DIM)
    value_fresh = value_all.reshape(step_count, req_count, heads_here, HEAD_DIM)
    cache_top, cache_total, cache_acc = local_attention(
        queries, k_cache, v_cache, lengths, slot_request, slot_page
    )
    holders = lax.axis_size("pages")
    myself = lax.axis_index("pages")
    group = req_count // holders
    packed = jnp.concatenate(
        [cache_acc, cache_total[..., None], cache_top[..., None]], axis=-1
    ).reshape(step_count, holders, group, heads_here, HEAD_DIM + 2)
    packed = jnp.moveaxis(packed, 1, 0)
    packed = lax.all_to_all(packed, "pages", split_axis=0, concat_axis=0, tiled=True)
    part_acc = packed[..., :HEAD_DIM]
    part_total = packed[..., HEAD_DIM]
    part_top = packed[..., HEAD_DIM + 1]
    mine = lambda a: lax.dynamic_slice_in_dim(a, myself * group, group, 1)
    queries_mine = mine(queries)
    key_mine = mine(key_fresh)
    value_mine = mine(value_fresh)
    scale = HEAD_DIM ** (-0.5)
    step_ids = jnp.arange(step_count, dtype=jnp.int32)
    causal = (step_ids[:, None] >= step_ids[None, :])[:, :, None, None]
    fresh = (
        jnp.einsum("trhd,urhd->turh", queries_mine, key_mine, preferred_element_type=jnp.float32)
        * scale
    )
    fresh = jnp.where(causal, fresh, NEGATIVE)
    row_top = jnp.maximum(jnp.max(part_top, axis=0), jnp.max(fresh, axis=1))
    carried = jnp.exp(part_top - row_top[None])
    fresh_w = jnp.where(causal, jnp.exp(fresh - row_top[:, None]), 0.0)
    totals = jnp.sum(part_total * carried, axis=0) + jnp.sum(fresh_w, axis=1)
    accums = jnp.sum(part_acc * carried[..., None], axis=0) + jnp.einsum(
        "turh,urhd->trhd",
        fresh_w.astype(jnp.bfloat16),
        value_mine,
        preferred_element_type=jnp.float32,
    )
    attended_mine = (accums / totals[..., None]).astype(jnp.bfloat16)
    attended = jnp.moveaxis(gather_blocks(attended_mine, "pages"), 0, 1).reshape(
        row_count, heads_here * HEAD_DIM
    )
    mixed = activ + across_heads(
        lax.dot_general(attended, w_out, CONTRACT_LAST, preferred_element_type=jnp.float32)
    )
    normed_two = (mixed * norm_gains[1]).astype(jnp.bfloat16)
    partial_two = jnp.einsum(
        "bd,gdf->bgf", normed_two, w_gate_up, preferred_element_type=jnp.float32
    )
    squares_two = jnp.sum(mixed * mixed, axis=1)
    (hidden,) = reduce_rows(partial_two, squares_two, finish_mlp)
    feed = across_heads(
        lax.dot_general(hidden, w_down, CONTRACT_LAST, preferred_element_type=jnp.float32)
    )
    layer_out = (mixed + feed).astype(jnp.bfloat16).reshape(step_count, req_count, width_here)
    new_k_cache, new_v_cache = land_pool(k_cache, v_cache, *received, move_slot, move_offset)
    return (layer_out, new_k_cache, new_v_cache)


def solution(mesh):
    in_specs = (
        P(None, None, "pages"),
        P(None, "pages"),
        P("pages", None, "mp"),
        P("pages", "mp"),
        P(None, "pages", "mp"),
        P("pages", "mp"),
        P("pages", None, "mp"),
        P("pages", None, "mp"),
        P(),
        P(),
        P(),
        P(),
        P(),
    )
    out_specs = (P(None, None, "pages"), P("pages", None, "mp"), P("pages", None, "mp"))
    return jax.shard_map(shards, mesh=mesh, in_specs=in_specs, out_specs=out_specs, check_vma=False)
```

```python
import jax
import jax.numpy as jnp
from jax import lax
from jax.sharding import PartitionSpec as P

D = 3072
HEAD_DIM = 96


EPSILON = 1e-05
NEGATIVE = -1e30
THETA = 10000.0
CONTRACT_LAST = (((1,), (1,)), ((), ()))


def merged(part, axis, combine):
    gathered = jax.tree.map(lambda a: lax.all_gather(a, axis), part)

    def take(source):
        return jax.tree.map(lambda a: lax.dynamic_index_in_dim(a, source, 0, False), gathered)

    return lax.fori_loop(
        1, lax.axis_size(axis), lambda source, state: combine(state, take(source)), take(0)
    )


def rotate(values, positions):
    half_dim = values.shape[-1] // 2
    exponent = jnp.arange(half_dim, dtype=jnp.float32) * (-2.0 / values.shape[-1])
    frequency = jnp.power(jnp.float32(THETA), exponent)
    angles = positions.astype(jnp.float32)[:, None, None] * frequency[None, None, :]
    cosine = jnp.cos(angles)
    sine = jnp.sin(angles)
    first = values[..., :half_dim]
    second = values[..., half_dim:]
    return jnp.concatenate(
        [first * cosine - second * sine, second * cosine + first * sine], axis=-1
    )


def merge_parts(first, second):
    top_a, total_a, accum_a = first
    top_b, total_b, accum_b = second
    joined = jnp.maximum(top_a, top_b)
    factor_a = jnp.exp(top_a - joined)
    factor_b = jnp.exp(top_b - joined)
    return (
        joined,
        total_a * factor_a + total_b * factor_b,
        accum_a * factor_a[..., None] + accum_b * factor_b[..., None],
    )


def reduce_rows(partial_value, squares, finish, tied=None):
    rows = partial_value.shape[0]
    packed = jnp.concatenate([partial_value.reshape(rows, -1), squares[:, None]], axis=1)
    packed = lax.psum(packed, "pages")
    if tied is not None:
        packed, tied = lax.optimization_barrier((packed, tied))
        return finish(packed[:, :-1].reshape(partial_value.shape), packed[:, -1], 0), tied
    total = packed[:, :-1].reshape(partial_value.shape)
    return finish(total, packed[:, -1], 0)


def gather_blocks(block, axis):
    count = lax.axis_size(axis)
    spread = jnp.broadcast_to(block[None], (count,) + block.shape)
    return lax.all_to_all(spread, axis, split_axis=0, concat_axis=0, tiled=True)


def across_heads(term):
    return jnp.sum(gather_blocks(term, "mp"), axis=0)


def migrate_pool(key_local, value_local, move_slot, move_offset):
    holders = lax.axis_size("pages")
    myself = lax.axis_index("pages")
    mine = lax.dynamic_index_in_dim(move_slot, myself, 0, keepdims=False)
    targets = (myself + move_offset) % holders
    holder_ids = jnp.arange(holders, dtype=jnp.int32)
    aimed = holder_ids[:, None] == targets[None, :]
    chosen = jnp.sum(jnp.where(aimed, mine[None, :], 0), axis=1)
    sending = jnp.any(aimed, axis=1)[:, None, None]
    key_send = jnp.where(sending, key_local[chosen], jnp.zeros((), key_local.dtype))
    value_send = jnp.where(sending, value_local[chosen], jnp.zeros((), value_local.dtype))
    return jnp.stack([key_send, value_send], axis=1)


def exchange_pool(both):
    both = lax.all_to_all(both, "pages", split_axis=0, concat_axis=0, tiled=True)
    return both[:, 0], both[:, 1]


def land_pool(key_local, value_local, key_recv, value_recv, move_slot, move_offset):
    holders = lax.axis_size("pages")
    myself = lax.axis_index("pages")
    mine = lax.dynamic_index_in_dim(move_slot, myself, 0, keepdims=False)
    sources = (myself - move_offset) % holders
    slot_ids = jnp.arange(key_local.shape[0], dtype=jnp.int32)
    landing = slot_ids[:, None] == mine[None, :]
    came_from = jnp.sum(jnp.where(landing, sources[None, :], 0), axis=1)
    arriving = jnp.any(landing, axis=1)[:, None, None]
    return (
        jnp.where(arriving, key_recv[came_from], key_local),
        jnp.where(arriving, value_recv[came_from], value_local),
    )


def local_attention(queries, k_cache, v_cache, lengths, slot_request, slot_page):
    step_count, req_count, heads_here, head_dim = queries.shape
    slot_count, page_len, channels = k_cache.shape
    scale = head_dim ** (-0.5)
    myself = lax.axis_index("pages")
    own_request = lax.dynamic_slice_in_dim(slot_request, myself * slot_count, slot_count)
    own_page = lax.dynamic_slice_in_dim(slot_page, myself * slot_count, slot_count)
    owners = jnp.clip(own_request, 0, req_count - 1)
    key_pos = own_page[:, None] * page_len + jnp.arange(page_len, dtype=jnp.int32)[None, :]
    usable = (own_request >= 0)[:, None] & (key_pos < lengths[owners][:, None])
    keys_here = k_cache.reshape(slot_count, page_len, heads_here, head_dim)
    values_here = v_cache.reshape(slot_count, page_len, heads_here, head_dim)
    scores = (
        jnp.einsum(
            "tshd,skhd->tshk", queries[:, owners], keys_here, preferred_element_type=jnp.float32
        )
        * scale
    )
    live_mask = usable[None, :, None, :]
    scores = jnp.where(live_mask, scores, NEGATIVE)
    slot_top = jnp.max(scores, axis=3)
    belongs = own_request[None, :] == jnp.arange(req_count, dtype=jnp.int32)[:, None]
    request_top = jnp.max(
        jnp.where(belongs[None, :, :, None], slot_top[:, None, :, :], NEGATIVE), axis=2
    )
    weights = jnp.where(live_mask, jnp.exp(scores - request_top[:, owners][..., None]), 0.0)
    slot_total = jnp.sum(weights, axis=3)
    slot_acc = jnp.einsum(
        "tshk,skhd->tshd",
        weights.astype(jnp.bfloat16),
        values_here,
        preferred_element_type=jnp.float32,
    )
    indicator = belongs.astype(jnp.float32)
    totals = jnp.einsum("rs,tsh->trh", indicator, slot_total, precision=lax.Precision.HIGHEST)
    accums = jnp.einsum("rs,tshd->trhd", indicator, slot_acc, precision=lax.Precision.HIGHEST)
    return (request_top, totals, accums)


def shards(
    tokens,
    norm_gains,
    w_qkv,
    w_out,
    w_gate_up,
    w_down,
    k_cache,
    v_cache,
    lengths,
    slot_request,
    slot_page,
    move_slot,
    move_offset,
):
    step_count, req_count, width_here = tokens.shape
    row_count = step_count * req_count
    activ = tokens.reshape(row_count, width_here).astype(jnp.float32)
    row_ids = jnp.arange(row_count, dtype=jnp.int32)
    positions = lengths[row_ids % req_count] + row_ids // req_count

    def finish_qkv(total, squares, start):
        count = total.shape[0]
        inverse = lax.rsqrt(squares / D + EPSILON)
        scaled = total * inverse[:, None, None]
        heads_here = scaled.shape[2] // HEAD_DIM
        query_rows = rotate(scaled[:, 0].reshape(count, heads_here, HEAD_DIM), positions)
        key_rows = rotate(scaled[:, 1].reshape(count, heads_here, HEAD_DIM), positions)
        return (
            query_rows.reshape(count, -1).astype(jnp.bfloat16),
            key_rows.reshape(count, -1).astype(jnp.bfloat16),
            scaled[:, 2].astype(jnp.bfloat16),
        )

    def finish_mlp(total, squares, start):
        inverse = lax.rsqrt(squares / D + EPSILON)
        gate = total[:, 0] * inverse[:, None]
        upward = total[:, 1] * inverse[:, None]
        return ((jax.nn.silu(gate) * upward).astype(jnp.bfloat16),)

    normed_one = (activ * norm_gains[0]).astype(jnp.bfloat16)
    partial_one = jnp.einsum("bd,dcn->bcn", normed_one, w_qkv, preferred_element_type=jnp.float32)
    squares_one = jnp.sum(activ * activ, axis=1)
    sending = migrate_pool(k_cache, v_cache, move_slot, move_offset)
    (query_all, key_all, value_all), sending = reduce_rows(
        partial_one, squares_one, finish_qkv, sending
    )
    heads_here = query_all.shape[1] // HEAD_DIM
    queries = query_all.reshape(step_count, req_count, heads_here, HEAD_DIM)
    key_fresh = key_all.reshape(step_count, req_count, heads_here, HEAD_DIM)
    value_fresh = value_all.reshape(step_count, req_count, heads_here, HEAD_DIM)
    cache_top, cache_total, cache_acc = local_attention(
        queries, k_cache, v_cache, lengths, slot_request, slot_page
    )
    holders = lax.axis_size("pages")
    myself = lax.axis_index("pages")
    group = req_count // holders
    packed = jnp.concatenate(
        [cache_acc, cache_total[..., None], cache_top[..., None]], axis=-1
    ).reshape(step_count, holders, group, heads_here, HEAD_DIM + 2)
    packed = jnp.moveaxis(packed, 1, 0)
    packed, received = lax.optimization_barrier((packed, exchange_pool(sending)))
    packed = lax.all_to_all(packed, "pages", split_axis=0, concat_axis=0, tiled=True)
    part_acc = packed[..., :HEAD_DIM]
    part_total = packed[..., HEAD_DIM]
    part_top = packed[..., HEAD_DIM + 1]
    mine = lambda a: lax.dynamic_slice_in_dim(a, myself * group, group, 1)
    queries_mine = mine(queries)
    key_mine = mine(key_fresh)
    value_mine = mine(value_fresh)
    scale = HEAD_DIM ** (-0.5)
    step_ids = jnp.arange(step_count, dtype=jnp.int32)
    causal = (step_ids[:, None] >= step_ids[None, :])[:, :, None, None]
    fresh = (
        jnp.einsum("trhd,urhd->turh", queries_mine, key_mine, preferred_element_type=jnp.float32)
        * scale
    )
    fresh = jnp.where(causal, fresh, NEGATIVE)
    row_top = jnp.maximum(jnp.max(part_top, axis=0), jnp.max(fresh, axis=1))
    carried = jnp.exp(part_top - row_top[None])
    fresh_w = jnp.where(causal, jnp.exp(fresh - row_top[:, None]), 0.0)
    totals = jnp.sum(part_total * carried, axis=0) + jnp.sum(fresh_w, axis=1)
    accums = jnp.sum(part_acc * carried[..., None], axis=0) + jnp.einsum(
        "turh,urhd->trhd",
        fresh_w.astype(jnp.bfloat16),
        value_mine,
        preferred_element_type=jnp.float32,
    )
    attended_mine = (accums / totals[..., None]).astype(jnp.bfloat16)
    attended = jnp.moveaxis(gather_blocks(attended_mine, "pages"), 0, 1).reshape(
        row_count, heads_here * HEAD_DIM
    )
    mixed = activ + across_heads(
        lax.dot_general(attended, w_out, CONTRACT_LAST, preferred_element_type=jnp.float32)
    )
    normed_two = (mixed * norm_gains[1]).astype(jnp.bfloat16)
    partial_two = jnp.einsum(
        "bd,gdf->bgf", normed_two, w_gate_up, preferred_element_type=jnp.float32
    )
    squares_two = jnp.sum(mixed * mixed, axis=1)
    (hidden,) = reduce_rows(partial_two, squares_two, finish_mlp)
    feed = across_heads(
        lax.dot_general(hidden, w_down, CONTRACT_LAST, preferred_element_type=jnp.float32)
    )
    layer_out = (mixed + feed).astype(jnp.bfloat16).reshape(step_count, req_count, width_here)
    new_k_cache, new_v_cache = land_pool(k_cache, v_cache, *received, move_slot, move_offset)
    return (layer_out, new_k_cache, new_v_cache)


def solution(mesh):
    in_specs = (
        P(None, None, "pages"),
        P(None, "pages"),
        P("pages", None, "mp"),
        P("pages", "mp"),
        P(None, "pages", "mp"),
        P("pages", "mp"),
        P("pages", None, "mp"),
        P("pages", None, "mp"),
        P(),
        P(),
        P(),
        P(),
        P(),
    )
    out_specs = (P(None, None, "pages"), P("pages", None, "mp"), P("pages", None, "mp"))
    return jax.shard_map(shards, mesh=mesh, in_specs=in_specs, out_specs=out_specs, check_vma=False)
```

```python
import jax
import jax.numpy as jnp
from jax import lax
from jax.sharding import PartitionSpec as P

D = 3072
HEAD_DIM = 96


EPSILON = 1e-05
NEGATIVE = -1e30
THETA = 10000.0
CONTRACT_LAST = (((1,), (1,)), ((), ()))


def merged(part, axis, combine):
    gathered = jax.tree.map(lambda a: lax.all_gather(a, axis), part)

    def take(source):
        return jax.tree.map(lambda a: lax.dynamic_index_in_dim(a, source, 0, False), gathered)

    return lax.fori_loop(
        1, lax.axis_size(axis), lambda source, state: combine(state, take(source)), take(0)
    )


def rotate(values, positions):
    half_dim = values.shape[-1] // 2
    exponent = jnp.arange(half_dim, dtype=jnp.float32) * (-2.0 / values.shape[-1])
    frequency = jnp.power(jnp.float32(THETA), exponent)
    angles = positions.astype(jnp.float32)[:, None, None] * frequency[None, None, :]
    cosine = jnp.cos(angles)
    sine = jnp.sin(angles)
    first = values[..., :half_dim]
    second = values[..., half_dim:]
    return jnp.concatenate(
        [first * cosine - second * sine, second * cosine + first * sine], axis=-1
    )


def merge_parts(first, second):
    top_a, total_a, accum_a = first
    top_b, total_b, accum_b = second
    joined = jnp.maximum(top_a, top_b)
    factor_a = jnp.exp(top_a - joined)
    factor_b = jnp.exp(top_b - joined)
    return (
        joined,
        total_a * factor_a + total_b * factor_b,
        accum_a * factor_a[..., None] + accum_b * factor_b[..., None],
    )


def reduce_rows(partial_value, squares, finish, tied=None):
    rows = partial_value.shape[0]
    holders = lax.axis_size("pages")
    block = rows // holders
    packed = jnp.concatenate([partial_value.reshape(rows, -1), squares[:, None]], axis=1)
    packed = packed.reshape(holders, block, packed.shape[1])
    packed = lax.all_to_all(packed, "pages", split_axis=0, concat_axis=0, tiled=True)
    packed = jnp.sum(packed, axis=0)
    start = lax.axis_index("pages") * block
    done = finish(packed[:, :-1].reshape((block,) + partial_value.shape[1:]), packed[:, -1], start)
    width = [part.shape[1] for part in done]
    joined = gather_blocks(jnp.concatenate(done, axis=1), "pages").reshape(rows, sum(width))
    pieces = []
    offset = 0
    for size in width:
        pieces.append(joined[:, offset : offset + size])
        offset += size
    if tied is not None:
        return lax.optimization_barrier((tuple(pieces), tied))
    return tuple(pieces)


def gather_blocks(block, axis):
    count = lax.axis_size(axis)
    spread = jnp.broadcast_to(block[None], (count,) + block.shape)
    return lax.all_to_all(spread, axis, split_axis=0, concat_axis=0, tiled=True)


def across_heads(term):
    return jnp.sum(gather_blocks(term, "mp"), axis=0)


def migrate_pool(key_local, value_local, move_slot, move_offset):
    holders = lax.axis_size("pages")
    myself = lax.axis_index("pages")
    mine = lax.dynamic_index_in_dim(move_slot, myself, 0, keepdims=False)
    targets = (myself + move_offset) % holders
    holder_ids = jnp.arange(holders, dtype=jnp.int32)
    aimed = holder_ids[:, None] == targets[None, :]
    chosen = jnp.sum(jnp.where(aimed, mine[None, :], 0), axis=1)
    sending = jnp.any(aimed, axis=1)[:, None, None]
    key_send = jnp.where(sending, key_local[chosen], jnp.zeros((), key_local.dtype))
    value_send = jnp.where(sending, value_local[chosen], jnp.zeros((), value_local.dtype))
    return jnp.stack([key_send, value_send], axis=1)


def exchange_pool(both):
    both = lax.all_to_all(both, "pages", split_axis=0, concat_axis=0, tiled=True)
    return both[:, 0], both[:, 1]


def land_pool(key_local, value_local, key_recv, value_recv, move_slot, move_offset):
    holders = lax.axis_size("pages")
    myself = lax.axis_index("pages")
    mine = lax.dynamic_index_in_dim(move_slot, myself, 0, keepdims=False)
    sources = (myself - move_offset) % holders
    slot_ids = jnp.arange(key_local.shape[0], dtype=jnp.int32)
    landing = slot_ids[:, None] == mine[None, :]
    came_from = jnp.sum(jnp.where(landing, sources[None, :], 0), axis=1)
    arriving = jnp.any(landing, axis=1)[:, None, None]
    return (
        jnp.where(arriving, key_recv[came_from], key_local),
        jnp.where(arriving, value_recv[came_from], value_local),
    )


def local_attention(queries, k_cache, v_cache, lengths, slot_request, slot_page):
    step_count, req_count, heads_here, head_dim = queries.shape
    slot_count, page_len, channels = k_cache.shape
    scale = head_dim ** (-0.5)
    myself = lax.axis_index("pages")
    own_request = lax.dynamic_slice_in_dim(slot_request, myself * slot_count, slot_count)
    own_page = lax.dynamic_slice_in_dim(slot_page, myself * slot_count, slot_count)
    owners = jnp.clip(own_request, 0, req_count - 1)
    key_pos = own_page[:, None] * page_len + jnp.arange(page_len, dtype=jnp.int32)[None, :]
    usable = (own_request >= 0)[:, None] & (key_pos < lengths[owners][:, None])
    keys_here = k_cache.reshape(slot_count, page_len, heads_here, head_dim)
    values_here = v_cache.reshape(slot_count, page_len, heads_here, head_dim)
    scores = (
        jnp.einsum(
            "tshd,skhd->tshk", queries[:, owners], keys_here, preferred_element_type=jnp.float32
        )
        * scale
    )
    live_mask = usable[None, :, None, :]
    scores = jnp.where(live_mask, scores, NEGATIVE)
    slot_top = jnp.max(scores, axis=3)
    belongs = own_request[None, :] == jnp.arange(req_count, dtype=jnp.int32)[:, None]
    request_top = jnp.max(
        jnp.where(belongs[None, :, :, None], slot_top[:, None, :, :], NEGATIVE), axis=2
    )
    weights = jnp.where(live_mask, jnp.exp(scores - request_top[:, owners][..., None]), 0.0)
    slot_total = jnp.sum(weights, axis=3)
    slot_acc = jnp.einsum(
        "tshk,skhd->tshd",
        weights.astype(jnp.bfloat16),
        values_here,
        preferred_element_type=jnp.float32,
    )
    indicator = belongs.astype(jnp.float32)
    totals = jnp.einsum("rs,tsh->trh", indicator, slot_total, precision=lax.Precision.HIGHEST)
    accums = jnp.einsum("rs,tshd->trhd", indicator, slot_acc, precision=lax.Precision.HIGHEST)
    return (request_top, totals, accums)


def shards(
    tokens,
    norm_gains,
    w_qkv,
    w_out,
    w_gate_up,
    w_down,
    k_cache,
    v_cache,
    lengths,
    slot_request,
    slot_page,
    move_slot,
    move_offset,
):
    step_count, req_count, width_here = tokens.shape
    row_count = step_count * req_count
    activ = tokens.reshape(row_count, width_here).astype(jnp.float32)
    row_ids = jnp.arange(row_count, dtype=jnp.int32)
    positions = lengths[row_ids % req_count] + row_ids // req_count

    def finish_qkv(total, squares, start):
        count = total.shape[0]
        rows_here = lax.dynamic_slice_in_dim(positions, start, count)
        inverse = lax.rsqrt(squares / D + EPSILON)
        scaled = total * inverse[:, None, None]
        heads_here = scaled.shape[2] // HEAD_DIM
        query_rows = rotate(scaled[:, 0].reshape(count, heads_here, HEAD_DIM), rows_here)
        key_rows = rotate(scaled[:, 1].reshape(count, heads_here, HEAD_DIM), rows_here)
        return (
            query_rows.reshape(count, -1).astype(jnp.bfloat16),
            key_rows.reshape(count, -1).astype(jnp.bfloat16),
            scaled[:, 2].astype(jnp.bfloat16),
        )

    def finish_mlp(total, squares, start):
        inverse = lax.rsqrt(squares / D + EPSILON)
        gate = total[:, 0] * inverse[:, None]
        upward = total[:, 1] * inverse[:, None]
        return ((jax.nn.silu(gate) * upward).astype(jnp.bfloat16),)

    normed_one = (activ * norm_gains[0]).astype(jnp.bfloat16)
    partial_one = jnp.einsum("bd,dcn->bcn", normed_one, w_qkv, preferred_element_type=jnp.float32)
    squares_one = jnp.sum(activ * activ, axis=1)
    sending = migrate_pool(k_cache, v_cache, move_slot, move_offset)
    (query_all, key_all, value_all), sending = reduce_rows(
        partial_one, squares_one, finish_qkv, sending
    )
    heads_here = query_all.shape[1] // HEAD_DIM
    queries = query_all.reshape(step_count, req_count, heads_here, HEAD_DIM)
    key_fresh = key_all.reshape(step_count, req_count, heads_here, HEAD_DIM)
    value_fresh = value_all.reshape(step_count, req_count, heads_here, HEAD_DIM)
    cache_top, cache_total, cache_acc = local_attention(
        queries, k_cache, v_cache, lengths, slot_request, slot_page
    )
    holders = lax.axis_size("pages")
    myself = lax.axis_index("pages")
    group = req_count // holders
    packed = jnp.concatenate(
        [cache_acc, cache_total[..., None], cache_top[..., None]], axis=-1
    ).reshape(step_count, holders, group, heads_here, HEAD_DIM + 2)
    packed = jnp.moveaxis(packed, 1, 0)
    packed, received = lax.optimization_barrier((packed, exchange_pool(sending)))
    packed = lax.all_to_all(packed, "pages", split_axis=0, concat_axis=0, tiled=True)
    part_acc = packed[..., :HEAD_DIM]
    part_total = packed[..., HEAD_DIM]
    part_top = packed[..., HEAD_DIM + 1]
    mine = lambda a: lax.dynamic_slice_in_dim(a, myself * group, group, 1)
    queries_mine = mine(queries)
    key_mine = mine(key_fresh)
    value_mine = mine(value_fresh)
    scale = HEAD_DIM ** (-0.5)
    step_ids = jnp.arange(step_count, dtype=jnp.int32)
    causal = (step_ids[:, None] >= step_ids[None, :])[:, :, None, None]
    fresh = (
        jnp.einsum("trhd,urhd->turh", queries_mine, key_mine, preferred_element_type=jnp.float32)
        * scale
    )
    fresh = jnp.where(causal, fresh, NEGATIVE)
    row_top = jnp.maximum(jnp.max(part_top, axis=0), jnp.max(fresh, axis=1))
    carried = jnp.exp(part_top - row_top[None])
    fresh_w = jnp.where(causal, jnp.exp(fresh - row_top[:, None]), 0.0)
    totals = jnp.sum(part_total * carried, axis=0) + jnp.sum(fresh_w, axis=1)
    accums = jnp.sum(part_acc * carried[..., None], axis=0) + jnp.einsum(
        "turh,urhd->trhd",
        fresh_w.astype(jnp.bfloat16),
        value_mine,
        preferred_element_type=jnp.float32,
    )
    attended_mine = (accums / totals[..., None]).astype(jnp.bfloat16)
    attended = jnp.moveaxis(gather_blocks(attended_mine, "pages"), 0, 1).reshape(
        row_count, heads_here * HEAD_DIM
    )
    mixed = activ + across_heads(
        lax.dot_general(attended, w_out, CONTRACT_LAST, preferred_element_type=jnp.float32)
    )
    normed_two = (mixed * norm_gains[1]).astype(jnp.bfloat16)
    partial_two = jnp.einsum(
        "bd,gdf->bgf", normed_two, w_gate_up, preferred_element_type=jnp.float32
    )
    squares_two = jnp.sum(mixed * mixed, axis=1)
    (hidden,) = reduce_rows(partial_two, squares_two, finish_mlp)
    feed = across_heads(
        lax.dot_general(hidden, w_down, CONTRACT_LAST, preferred_element_type=jnp.float32)
    )
    layer_out = (mixed + feed).astype(jnp.bfloat16).reshape(step_count, req_count, width_here)
    new_k_cache, new_v_cache = land_pool(k_cache, v_cache, *received, move_slot, move_offset)
    return (layer_out, new_k_cache, new_v_cache)


def solution(mesh):
    in_specs = (
        P(None, None, "pages"),
        P(None, "pages"),
        P("pages", None, "mp"),
        P("pages", "mp"),
        P(None, "pages", "mp"),
        P("pages", "mp"),
        P("pages", None, "mp"),
        P("pages", None, "mp"),
        P(),
        P(),
        P(),
        P(),
        P(),
    )
    out_specs = (P(None, None, "pages"), P("pages", None, "mp"), P("pages", None, "mp"))
    return jax.shard_map(shards, mesh=mesh, in_specs=in_specs, out_specs=out_specs, check_vma=False)
```

```python
import jax
import jax.numpy as jnp
from jax import lax
from jax.sharding import PartitionSpec as P

D = 3072
HEAD_DIM = 96


EPSILON = 1e-05
NEGATIVE = -1e30
THETA = 10000.0
CONTRACT_LAST = (((1,), (1,)), ((), ()))


def merged(part, axis, combine):
    gathered = jax.tree.map(lambda a: lax.all_gather(a, axis), part)

    def take(source):
        return jax.tree.map(lambda a: lax.dynamic_index_in_dim(a, source, 0, False), gathered)

    return lax.fori_loop(
        1, lax.axis_size(axis), lambda source, state: combine(state, take(source)), take(0)
    )


def rotate(values, positions):
    half_dim = values.shape[-1] // 2
    exponent = jnp.arange(half_dim, dtype=jnp.float32) * (-2.0 / values.shape[-1])
    frequency = jnp.power(jnp.float32(THETA), exponent)
    angles = positions.astype(jnp.float32)[:, None, None] * frequency[None, None, :]
    cosine = jnp.cos(angles)
    sine = jnp.sin(angles)
    first = values[..., :half_dim]
    second = values[..., half_dim:]
    return jnp.concatenate(
        [first * cosine - second * sine, second * cosine + first * sine], axis=-1
    )


def merge_parts(first, second):
    top_a, total_a, accum_a = first
    top_b, total_b, accum_b = second
    joined = jnp.maximum(top_a, top_b)
    factor_a = jnp.exp(top_a - joined)
    factor_b = jnp.exp(top_b - joined)
    return (
        joined,
        total_a * factor_a + total_b * factor_b,
        accum_a * factor_a[..., None] + accum_b * factor_b[..., None],
    )


def reduce_rows(partial_value, squares, finish, tied=None):
    rows = partial_value.shape[0]
    holders = lax.axis_size("pages")
    block = rows // holders
    packed = jnp.concatenate([partial_value.reshape(rows, -1), squares[:, None]], axis=1)
    packed = packed.reshape(holders, block, packed.shape[1])
    packed = lax.all_to_all(packed, "pages", split_axis=0, concat_axis=0, tiled=True)
    packed = jnp.sum(packed, axis=0)
    start = lax.axis_index("pages") * block
    done = finish(packed[:, :-1].reshape((block,) + partial_value.shape[1:]), packed[:, -1], start)
    width = [part.shape[1] for part in done]
    joined = gather_blocks(jnp.concatenate(done, axis=1), "pages").reshape(rows, sum(width))
    pieces = []
    offset = 0
    for size in width:
        pieces.append(joined[:, offset : offset + size])
        offset += size
    if tied is not None:
        return lax.optimization_barrier((tuple(pieces), tied))
    return tuple(pieces)


def gather_blocks(block, axis):
    count = lax.axis_size(axis)
    spread = jnp.broadcast_to(block[None], (count,) + block.shape)
    return lax.all_to_all(spread, axis, split_axis=0, concat_axis=0, tiled=True)


def across_heads(term):
    return jnp.sum(gather_blocks(term, "mp"), axis=0)


def migrate_pool(key_local, value_local, move_slot, move_offset):
    holders = lax.axis_size("pages")
    myself = lax.axis_index("pages")
    mine = lax.dynamic_index_in_dim(move_slot, myself, 0, keepdims=False)
    arrived = []
    for shift in range(1, holders):
        move = jnp.argmax(move_offset == shift)
        slot = mine[move]
        page = jnp.stack([key_local[slot], value_local[slot]])
        ring = [(source, (source + shift) % holders) for source in range(holders)]
        arrived.append(lax.ppermute(page, "pages", ring))
    return jnp.stack(arrived)


def land_pool(key_local, value_local, arrived, move_slot, move_offset):
    myself = lax.axis_index("pages")
    mine = lax.dynamic_index_in_dim(move_slot, myself, 0, keepdims=False)
    slot_ids = jnp.arange(key_local.shape[0], dtype=jnp.int32)
    landing = slot_ids[:, None] == mine[None, :]
    came_from = jnp.sum(jnp.where(landing, move_offset[None, :] - 1, 0), axis=1)
    arriving = jnp.any(landing, axis=1)[:, None, None]
    picked = arrived[came_from]
    return (
        jnp.where(arriving, picked[:, 0], key_local),
        jnp.where(arriving, picked[:, 1], value_local),
    )


def local_attention(queries, k_cache, v_cache, lengths, slot_request, slot_page):
    step_count, req_count, heads_here, head_dim = queries.shape
    slot_count, page_len, channels = k_cache.shape
    scale = head_dim ** (-0.5)
    myself = lax.axis_index("pages")
    own_request = lax.dynamic_slice_in_dim(slot_request, myself * slot_count, slot_count)
    own_page = lax.dynamic_slice_in_dim(slot_page, myself * slot_count, slot_count)
    owners = jnp.clip(own_request, 0, req_count - 1)
    key_pos = own_page[:, None] * page_len + jnp.arange(page_len, dtype=jnp.int32)[None, :]
    usable = (own_request >= 0)[:, None] & (key_pos < lengths[owners][:, None])
    keys_here = k_cache.reshape(slot_count, page_len, heads_here, head_dim)
    values_here = v_cache.reshape(slot_count, page_len, heads_here, head_dim)
    scores = (
        jnp.einsum(
            "tshd,skhd->tshk", queries[:, owners], keys_here, preferred_element_type=jnp.float32
        )
        * scale
    )
    live_mask = usable[None, :, None, :]
    scores = jnp.where(live_mask, scores, NEGATIVE)
    slot_top = jnp.max(scores, axis=3)
    belongs = own_request[None, :] == jnp.arange(req_count, dtype=jnp.int32)[:, None]
    request_top = jnp.max(
        jnp.where(belongs[None, :, :, None], slot_top[:, None, :, :], NEGATIVE), axis=2
    )
    weights = jnp.where(live_mask, jnp.exp(scores - request_top[:, owners][..., None]), 0.0)
    slot_total = jnp.sum(weights, axis=3)
    slot_acc = jnp.einsum(
        "tshk,skhd->tshd",
        weights.astype(jnp.bfloat16),
        values_here,
        preferred_element_type=jnp.float32,
    )
    indicator = belongs.astype(jnp.float32)
    totals = jnp.einsum("rs,tsh->trh", indicator, slot_total, precision=lax.Precision.HIGHEST)
    accums = jnp.einsum("rs,tshd->trhd", indicator, slot_acc, precision=lax.Precision.HIGHEST)
    return (request_top, totals, accums)


def shards(
    tokens,
    norm_gains,
    w_qkv,
    w_out,
    w_gate_up,
    w_down,
    k_cache,
    v_cache,
    lengths,
    slot_request,
    slot_page,
    move_slot,
    move_offset,
):
    step_count, req_count, width_here = tokens.shape
    row_count = step_count * req_count
    activ = tokens.reshape(row_count, width_here).astype(jnp.float32)
    row_ids = jnp.arange(row_count, dtype=jnp.int32)
    positions = lengths[row_ids % req_count] + row_ids // req_count

    def finish_qkv(total, squares, start):
        count = total.shape[0]
        rows_here = lax.dynamic_slice_in_dim(positions, start, count)
        inverse = lax.rsqrt(squares / D + EPSILON)
        scaled = total * inverse[:, None, None]
        heads_here = scaled.shape[2] // HEAD_DIM
        query_rows = rotate(scaled[:, 0].reshape(count, heads_here, HEAD_DIM), rows_here)
        key_rows = rotate(scaled[:, 1].reshape(count, heads_here, HEAD_DIM), rows_here)
        return (
            query_rows.reshape(count, -1).astype(jnp.bfloat16),
            key_rows.reshape(count, -1).astype(jnp.bfloat16),
            scaled[:, 2].astype(jnp.bfloat16),
        )

    def finish_mlp(total, squares, start):
        inverse = lax.rsqrt(squares / D + EPSILON)
        gate = total[:, 0] * inverse[:, None]
        upward = total[:, 1] * inverse[:, None]
        return ((jax.nn.silu(gate) * upward).astype(jnp.bfloat16),)

    normed_one = (activ * norm_gains[0]).astype(jnp.bfloat16)
    partial_one = jnp.einsum("bd,dcn->bcn", normed_one, w_qkv, preferred_element_type=jnp.float32)
    squares_one = jnp.sum(activ * activ, axis=1)
    query_all, key_all, value_all = reduce_rows(partial_one, squares_one, finish_qkv)
    heads_here = query_all.shape[1] // HEAD_DIM
    queries = query_all.reshape(step_count, req_count, heads_here, HEAD_DIM)
    key_fresh = key_all.reshape(step_count, req_count, heads_here, HEAD_DIM)
    value_fresh = value_all.reshape(step_count, req_count, heads_here, HEAD_DIM)
    cache_top, cache_total, cache_acc = local_attention(
        queries, k_cache, v_cache, lengths, slot_request, slot_page
    )
    holders = lax.axis_size("pages")
    myself = lax.axis_index("pages")
    group = req_count // holders
    packed = jnp.concatenate(
        [cache_acc, cache_total[..., None], cache_top[..., None]], axis=-1
    ).reshape(step_count, holders, group, heads_here, HEAD_DIM + 2)
    packed = jnp.moveaxis(packed, 1, 0)
    packed = lax.all_to_all(packed, "pages", split_axis=0, concat_axis=0, tiled=True)
    part_acc = packed[..., :HEAD_DIM]
    part_total = packed[..., HEAD_DIM]
    part_top = packed[..., HEAD_DIM + 1]
    mine = lambda a: lax.dynamic_slice_in_dim(a, myself * group, group, 1)
    queries_mine = mine(queries)
    key_mine = mine(key_fresh)
    value_mine = mine(value_fresh)
    scale = HEAD_DIM ** (-0.5)
    step_ids = jnp.arange(step_count, dtype=jnp.int32)
    causal = (step_ids[:, None] >= step_ids[None, :])[:, :, None, None]
    fresh = (
        jnp.einsum("trhd,urhd->turh", queries_mine, key_mine, preferred_element_type=jnp.float32)
        * scale
    )
    fresh = jnp.where(causal, fresh, NEGATIVE)
    row_top = jnp.maximum(jnp.max(part_top, axis=0), jnp.max(fresh, axis=1))
    carried = jnp.exp(part_top - row_top[None])
    fresh_w = jnp.where(causal, jnp.exp(fresh - row_top[:, None]), 0.0)
    totals = jnp.sum(part_total * carried, axis=0) + jnp.sum(fresh_w, axis=1)
    accums = jnp.sum(part_acc * carried[..., None], axis=0) + jnp.einsum(
        "turh,urhd->trhd",
        fresh_w.astype(jnp.bfloat16),
        value_mine,
        preferred_element_type=jnp.float32,
    )
    attended_mine = (accums / totals[..., None]).astype(jnp.bfloat16)
    attended = jnp.moveaxis(gather_blocks(attended_mine, "pages"), 0, 1).reshape(
        row_count, heads_here * HEAD_DIM
    )
    mixed = activ + across_heads(
        lax.dot_general(attended, w_out, CONTRACT_LAST, preferred_element_type=jnp.float32)
    )
    normed_two = (mixed * norm_gains[1]).astype(jnp.bfloat16)
    partial_two = jnp.einsum(
        "bd,gdf->bgf", normed_two, w_gate_up, preferred_element_type=jnp.float32
    )
    squares_two = jnp.sum(mixed * mixed, axis=1)
    (hidden,) = reduce_rows(partial_two, squares_two, finish_mlp)
    feed = across_heads(
        lax.dot_general(hidden, w_down, CONTRACT_LAST, preferred_element_type=jnp.float32)
    )
    layer_out = (mixed + feed).astype(jnp.bfloat16).reshape(step_count, req_count, width_here)
    arrived = migrate_pool(k_cache, v_cache, move_slot, move_offset)
    new_k_cache, new_v_cache = land_pool(k_cache, v_cache, arrived, move_slot, move_offset)
    return (layer_out, new_k_cache, new_v_cache)


def solution(mesh):
    in_specs = (
        P(None, None, "pages"),
        P(None, "pages"),
        P("pages", None, "mp"),
        P("pages", "mp"),
        P(None, "pages", "mp"),
        P("pages", "mp"),
        P("pages", None, "mp"),
        P("pages", None, "mp"),
        P(),
        P(),
        P(),
        P(),
        P(),
    )
    out_specs = (P(None, None, "pages"), P("pages", None, "mp"), P("pages", None, "mp"))
    return jax.shard_map(shards, mesh=mesh, in_specs=in_specs, out_specs=out_specs, check_vma=False)
```

```python
import jax
import jax.numpy as jnp
from jax import lax
from jax.sharding import PartitionSpec as P

D = 3072
HEAD_DIM = 96


EPSILON = 1e-05
NEGATIVE = -1e30
THETA = 10000.0
CONTRACT_LAST = (((1,), (1,)), ((), ()))


def merged(part, axis, combine):
    gathered = jax.tree.map(lambda a: lax.all_gather(a, axis), part)

    def take(source):
        return jax.tree.map(lambda a: lax.dynamic_index_in_dim(a, source, 0, False), gathered)

    return lax.fori_loop(
        1, lax.axis_size(axis), lambda source, state: combine(state, take(source)), take(0)
    )


def rotate(values, positions):
    half_dim = values.shape[-1] // 2
    exponent = jnp.arange(half_dim, dtype=jnp.float32) * (-2.0 / values.shape[-1])
    frequency = jnp.power(jnp.float32(THETA), exponent)
    angles = positions.astype(jnp.float32)[:, None, None] * frequency[None, None, :]
    cosine = jnp.cos(angles)
    sine = jnp.sin(angles)
    first = values[..., :half_dim]
    second = values[..., half_dim:]
    return jnp.concatenate(
        [first * cosine - second * sine, second * cosine + first * sine], axis=-1
    )


def merge_parts(first, second):
    top_a, total_a, accum_a = first
    top_b, total_b, accum_b = second
    joined = jnp.maximum(top_a, top_b)
    factor_a = jnp.exp(top_a - joined)
    factor_b = jnp.exp(top_b - joined)
    return (
        joined,
        total_a * factor_a + total_b * factor_b,
        accum_a * factor_a[..., None] + accum_b * factor_b[..., None],
    )


def reduce_rows(partial_value, squares, finish, tied=None, carrier=jnp.float32):
    rows = partial_value.shape[0]
    holders = lax.axis_size("pages")
    block = rows // holders
    packed = jnp.concatenate([partial_value.reshape(rows, -1), squares[:, None]], axis=1)
    packed = packed.reshape(holders, block, packed.shape[1]).astype(carrier)
    packed = lax.all_to_all(packed, "pages", split_axis=0, concat_axis=0, tiled=True)
    packed = jnp.sum(packed.astype(jnp.float32), axis=0)
    start = lax.axis_index("pages") * block
    done = finish(packed[:, :-1].reshape((block,) + partial_value.shape[1:]), packed[:, -1], start)
    width = [part.shape[1] for part in done]
    joined = gather_blocks(jnp.concatenate(done, axis=1), "pages").reshape(rows, sum(width))
    pieces = []
    offset = 0
    for size in width:
        pieces.append(joined[:, offset : offset + size])
        offset += size
    if tied is not None:
        return lax.optimization_barrier((tuple(pieces), tied))
    return tuple(pieces)


def gather_blocks(block, axis):
    count = lax.axis_size(axis)
    spread = jnp.broadcast_to(block[None], (count,) + block.shape)
    return lax.all_to_all(spread, axis, split_axis=0, concat_axis=0, tiled=True)


def across_heads(term):
    return jnp.sum(gather_blocks(term, "mp"), axis=0)


def migrate_pool(key_local, value_local, move_slot, move_offset):
    holders = lax.axis_size("pages")
    myself = lax.axis_index("pages")
    mine = lax.dynamic_index_in_dim(move_slot, myself, 0, keepdims=False)
    targets = (myself + move_offset) % holders
    holder_ids = jnp.arange(holders, dtype=jnp.int32)
    aimed = holder_ids[:, None] == targets[None, :]
    chosen = jnp.sum(jnp.where(aimed, mine[None, :], 0), axis=1)
    sending = jnp.any(aimed, axis=1)[:, None, None]
    key_send = jnp.where(sending, key_local[chosen], jnp.zeros((), key_local.dtype))
    value_send = jnp.where(sending, value_local[chosen], jnp.zeros((), value_local.dtype))
    return jnp.stack([key_send, value_send], axis=1)


def exchange_pool(both):
    both = lax.all_to_all(both, "pages", split_axis=0, concat_axis=0, tiled=True)
    return both[:, 0], both[:, 1]


def land_pool(key_local, value_local, key_recv, value_recv, move_slot, move_offset):
    holders = lax.axis_size("pages")
    myself = lax.axis_index("pages")
    mine = lax.dynamic_index_in_dim(move_slot, myself, 0, keepdims=False)
    sources = (myself - move_offset) % holders
    slot_ids = jnp.arange(key_local.shape[0], dtype=jnp.int32)
    landing = slot_ids[:, None] == mine[None, :]
    came_from = jnp.sum(jnp.where(landing, sources[None, :], 0), axis=1)
    arriving = jnp.any(landing, axis=1)[:, None, None]
    return (
        jnp.where(arriving, key_recv[came_from], key_local),
        jnp.where(arriving, value_recv[came_from], value_local),
    )


def local_attention(queries, k_cache, v_cache, lengths, slot_request, slot_page):
    step_count, req_count, heads_here, head_dim = queries.shape
    slot_count, page_len, channels = k_cache.shape
    scale = head_dim ** (-0.5)
    myself = lax.axis_index("pages")
    own_request = lax.dynamic_slice_in_dim(slot_request, myself * slot_count, slot_count)
    own_page = lax.dynamic_slice_in_dim(slot_page, myself * slot_count, slot_count)
    owners = jnp.clip(own_request, 0, req_count - 1)
    key_pos = own_page[:, None] * page_len + jnp.arange(page_len, dtype=jnp.int32)[None, :]
    usable = (own_request >= 0)[:, None] & (key_pos < lengths[owners][:, None])
    keys_here = k_cache.reshape(slot_count, page_len, heads_here, head_dim)
    values_here = v_cache.reshape(slot_count, page_len, heads_here, head_dim)
    scores = (
        jnp.einsum(
            "tshd,skhd->tshk", queries[:, owners], keys_here, preferred_element_type=jnp.float32
        )
        * scale
    )
    live_mask = usable[None, :, None, :]
    scores = jnp.where(live_mask, scores, NEGATIVE)
    slot_top = jnp.max(scores, axis=3)
    belongs = own_request[None, :] == jnp.arange(req_count, dtype=jnp.int32)[:, None]
    request_top = jnp.max(
        jnp.where(belongs[None, :, :, None], slot_top[:, None, :, :], NEGATIVE), axis=2
    )
    weights = jnp.where(live_mask, jnp.exp(scores - request_top[:, owners][..., None]), 0.0)
    slot_total = jnp.sum(weights, axis=3)
    slot_acc = jnp.einsum(
        "tshk,skhd->tshd",
        weights.astype(jnp.bfloat16),
        values_here,
        preferred_element_type=jnp.float32,
    )
    indicator = belongs.astype(jnp.float32)
    totals = jnp.einsum("rs,tsh->trh", indicator, slot_total, precision=lax.Precision.HIGHEST)
    accums = jnp.einsum("rs,tshd->trhd", indicator, slot_acc, precision=lax.Precision.HIGHEST)
    return (request_top, totals, accums)


def shards(
    tokens,
    norm_gains,
    w_qkv,
    w_out,
    w_gate_up,
    w_down,
    k_cache,
    v_cache,
    lengths,
    slot_request,
    slot_page,
    move_slot,
    move_offset,
):
    step_count, req_count, width_here = tokens.shape
    row_count = step_count * req_count
    activ = tokens.reshape(row_count, width_here).astype(jnp.float32)
    row_ids = jnp.arange(row_count, dtype=jnp.int32)
    positions = lengths[row_ids % req_count] + row_ids // req_count

    def finish_qkv(total, squares, start):
        count = total.shape[0]
        rows_here = lax.dynamic_slice_in_dim(positions, start, count)
        inverse = lax.rsqrt(squares / D + EPSILON)
        scaled = total * inverse[:, None, None]
        heads_here = scaled.shape[2] // HEAD_DIM
        query_rows = rotate(scaled[:, 0].reshape(count, heads_here, HEAD_DIM), rows_here)
        key_rows = rotate(scaled[:, 1].reshape(count, heads_here, HEAD_DIM), rows_here)
        return (
            query_rows.reshape(count, -1).astype(jnp.bfloat16),
            key_rows.reshape(count, -1).astype(jnp.bfloat16),
            scaled[:, 2].astype(jnp.bfloat16),
        )

    def finish_mlp(total, squares, start):
        inverse = lax.rsqrt(squares / D + EPSILON)
        gate = total[:, 0] * inverse[:, None]
        upward = total[:, 1] * inverse[:, None]
        return ((jax.nn.silu(gate) * upward).astype(jnp.bfloat16),)

    normed_one = (activ * norm_gains[0]).astype(jnp.bfloat16)
    partial_one = jnp.einsum("bd,dcn->bcn", normed_one, w_qkv, preferred_element_type=jnp.float32)
    squares_one = jnp.sum(activ * activ, axis=1)
    sending = migrate_pool(k_cache, v_cache, move_slot, move_offset)
    (query_all, key_all, value_all), sending = reduce_rows(
        partial_one, squares_one, finish_qkv, sending
    )
    heads_here = query_all.shape[1] // HEAD_DIM
    queries = query_all.reshape(step_count, req_count, heads_here, HEAD_DIM)
    key_fresh = key_all.reshape(step_count, req_count, heads_here, HEAD_DIM)
    value_fresh = value_all.reshape(step_count, req_count, heads_here, HEAD_DIM)
    cache_top, cache_total, cache_acc = local_attention(
        queries, k_cache, v_cache, lengths, slot_request, slot_page
    )
    holders = lax.axis_size("pages")
    myself = lax.axis_index("pages")
    group = req_count // holders
    packed = jnp.concatenate(
        [cache_acc, cache_total[..., None], cache_top[..., None]], axis=-1
    ).reshape(step_count, holders, group, heads_here, HEAD_DIM + 2)
    packed = jnp.moveaxis(packed, 1, 0)
    packed, received = lax.optimization_barrier((packed, exchange_pool(sending)))
    packed = lax.all_to_all(packed, "pages", split_axis=0, concat_axis=0, tiled=True)
    part_acc = packed[..., :HEAD_DIM]
    part_total = packed[..., HEAD_DIM]
    part_top = packed[..., HEAD_DIM + 1]
    mine = lambda a: lax.dynamic_slice_in_dim(a, myself * group, group, 1)
    queries_mine = mine(queries)
    key_mine = mine(key_fresh)
    value_mine = mine(value_fresh)
    scale = HEAD_DIM ** (-0.5)
    step_ids = jnp.arange(step_count, dtype=jnp.int32)
    causal = (step_ids[:, None] >= step_ids[None, :])[:, :, None, None]
    fresh = (
        jnp.einsum("trhd,urhd->turh", queries_mine, key_mine, preferred_element_type=jnp.float32)
        * scale
    )
    fresh = jnp.where(causal, fresh, NEGATIVE)
    row_top = jnp.maximum(jnp.max(part_top, axis=0), jnp.max(fresh, axis=1))
    carried = jnp.exp(part_top - row_top[None])
    fresh_w = jnp.where(causal, jnp.exp(fresh - row_top[:, None]), 0.0)
    totals = jnp.sum(part_total * carried, axis=0) + jnp.sum(fresh_w, axis=1)
    accums = jnp.sum(part_acc * carried[..., None], axis=0) + jnp.einsum(
        "turh,urhd->trhd",
        fresh_w.astype(jnp.bfloat16),
        value_mine,
        preferred_element_type=jnp.float32,
    )
    attended_mine = (accums / totals[..., None]).astype(jnp.bfloat16)
    attended = jnp.moveaxis(gather_blocks(attended_mine, "pages"), 0, 1).reshape(
        row_count, heads_here * HEAD_DIM
    )
    mixed = activ + across_heads(
        lax.dot_general(attended, w_out, CONTRACT_LAST, preferred_element_type=jnp.float32)
    )
    normed_two = (mixed * norm_gains[1]).astype(jnp.bfloat16)
    partial_two = jnp.einsum(
        "bd,gdf->bgf", normed_two, w_gate_up, preferred_element_type=jnp.float32
    )
    squares_two = jnp.sum(mixed * mixed, axis=1)
    (hidden,) = reduce_rows(partial_two, squares_two, finish_mlp, carrier=jnp.bfloat16)
    feed = across_heads(
        lax.dot_general(hidden, w_down, CONTRACT_LAST, preferred_element_type=jnp.float32)
    )
    layer_out = (mixed + feed).astype(jnp.bfloat16).reshape(step_count, req_count, width_here)
    new_k_cache, new_v_cache = land_pool(k_cache, v_cache, *received, move_slot, move_offset)
    return (layer_out, new_k_cache, new_v_cache)


def solution(mesh):
    in_specs = (
        P(None, None, "pages"),
        P(None, "pages"),
        P("pages", None, "mp"),
        P("pages", "mp"),
        P(None, "pages", "mp"),
        P("pages", "mp"),
        P("pages", None, "mp"),
        P("pages", None, "mp"),
        P(),
        P(),
        P(),
        P(),
        P(),
    )
    out_specs = (P(None, None, "pages"), P("pages", None, "mp"), P("pages", None, "mp"))
    return jax.shard_map(shards, mesh=mesh, in_specs=in_specs, out_specs=out_specs, check_vma=False)
```

```python
import jax
import jax.numpy as jnp
from jax import lax
from jax.sharding import PartitionSpec as P

D = 3072
HEAD_DIM = 96


EPSILON = 1e-05
NEGATIVE = -1e30
THETA = 10000.0
CONTRACT_LAST = (((1,), (1,)), ((), ()))


def merged(part, axis, combine):
    gathered = jax.tree.map(lambda a: lax.all_gather(a, axis), part)

    def take(source):
        return jax.tree.map(lambda a: lax.dynamic_index_in_dim(a, source, 0, False), gathered)

    return lax.fori_loop(
        1, lax.axis_size(axis), lambda source, state: combine(state, take(source)), take(0)
    )


def rotate(values, positions):
    half_dim = values.shape[-1] // 2
    exponent = jnp.arange(half_dim, dtype=jnp.float32) * (-2.0 / values.shape[-1])
    frequency = jnp.power(jnp.float32(THETA), exponent)
    angles = positions.astype(jnp.float32)[:, None, None] * frequency[None, None, :]
    cosine = jnp.cos(angles)
    sine = jnp.sin(angles)
    first = values[..., :half_dim]
    second = values[..., half_dim:]
    return jnp.concatenate(
        [first * cosine - second * sine, second * cosine + first * sine], axis=-1
    )


def merge_parts(first, second):
    top_a, total_a, accum_a = first
    top_b, total_b, accum_b = second
    joined = jnp.maximum(top_a, top_b)
    factor_a = jnp.exp(top_a - joined)
    factor_b = jnp.exp(top_b - joined)
    return (
        joined,
        total_a * factor_a + total_b * factor_b,
        accum_a * factor_a[..., None] + accum_b * factor_b[..., None],
    )


def reduce_rows(partial_value, squares, finish, tied=None, carrier=jnp.float32):
    rows = partial_value.shape[0]
    holders = lax.axis_size("pages")
    block = rows // holders
    packed = jnp.concatenate([partial_value.reshape(rows, -1), squares[:, None]], axis=1)
    packed = packed.reshape(holders, block, packed.shape[1]).astype(carrier)
    packed = lax.all_to_all(packed, "pages", split_axis=0, concat_axis=0, tiled=True)
    packed = jnp.sum(packed.astype(jnp.float32), axis=0)
    start = lax.axis_index("pages") * block
    done = finish(packed[:, :-1].reshape((block,) + partial_value.shape[1:]), packed[:, -1], start)
    width = [part.shape[1] for part in done]
    joined = gather_blocks(jnp.concatenate(done, axis=1), "pages").reshape(rows, sum(width))
    pieces = []
    offset = 0
    for size in width:
        pieces.append(joined[:, offset : offset + size])
        offset += size
    if tied is not None:
        return lax.optimization_barrier((tuple(pieces), tied))
    return tuple(pieces)


def gather_blocks(block, axis):
    count = lax.axis_size(axis)
    spread = jnp.broadcast_to(block[None], (count,) + block.shape)
    return lax.all_to_all(spread, axis, split_axis=0, concat_axis=0, tiled=True)


def across_heads(term):
    return jnp.sum(gather_blocks(term, "mp"), axis=0)


def migrate_pool(key_local, value_local, move_slot, move_offset):
    holders = lax.axis_size("pages")
    myself = lax.axis_index("pages")
    mine = lax.dynamic_index_in_dim(move_slot, myself, 0, keepdims=False)
    targets = (myself + move_offset) % holders
    holder_ids = jnp.arange(holders, dtype=jnp.int32)
    aimed = holder_ids[:, None] == targets[None, :]
    chosen = jnp.sum(jnp.where(aimed, mine[None, :], 0), axis=1)
    sending = jnp.any(aimed, axis=1)[:, None, None]
    key_send = jnp.where(sending, key_local[chosen], jnp.zeros((), key_local.dtype))
    value_send = jnp.where(sending, value_local[chosen], jnp.zeros((), value_local.dtype))
    return jnp.stack([key_send, value_send], axis=1)


def exchange_pool(both):
    both = lax.all_to_all(both, "pages", split_axis=0, concat_axis=0, tiled=True)
    return both[:, 0], both[:, 1]


def land_pool(key_local, value_local, key_recv, value_recv, move_slot, move_offset):
    holders = lax.axis_size("pages")
    myself = lax.axis_index("pages")
    mine = lax.dynamic_index_in_dim(move_slot, myself, 0, keepdims=False)
    sources = (myself - move_offset) % holders
    slot_ids = jnp.arange(key_local.shape[0], dtype=jnp.int32)
    landing = slot_ids[:, None] == mine[None, :]
    came_from = jnp.sum(jnp.where(landing, sources[None, :], 0), axis=1)
    arriving = jnp.any(landing, axis=1)[:, None, None]
    return (
        jnp.where(arriving, key_recv[came_from], key_local),
        jnp.where(arriving, value_recv[came_from], value_local),
    )


def local_attention(queries, k_cache, v_cache, lengths, slot_request, slot_page):
    step_count, req_count, heads_here, head_dim = queries.shape
    slot_count, page_len, channels = k_cache.shape
    scale = head_dim ** (-0.5)
    myself = lax.axis_index("pages")
    own_request = lax.dynamic_slice_in_dim(slot_request, myself * slot_count, slot_count)
    own_page = lax.dynamic_slice_in_dim(slot_page, myself * slot_count, slot_count)
    owners = jnp.clip(own_request, 0, req_count - 1)
    key_pos = own_page[:, None] * page_len + jnp.arange(page_len, dtype=jnp.int32)[None, :]
    usable = (own_request >= 0)[:, None] & (key_pos < lengths[owners][:, None])
    keys_here = k_cache.reshape(slot_count, page_len, heads_here, head_dim)
    values_here = v_cache.reshape(slot_count, page_len, heads_here, head_dim)
    scores = (
        jnp.einsum(
            "tshd,skhd->tshk", queries[:, owners], keys_here, preferred_element_type=jnp.float32
        )
        * scale
    )
    live_mask = usable[None, :, None, :]
    scores = jnp.where(live_mask, scores, NEGATIVE)
    slot_top = jnp.max(scores, axis=3)
    belongs = own_request[None, :] == jnp.arange(req_count, dtype=jnp.int32)[:, None]
    request_top = jnp.max(
        jnp.where(belongs[None, :, :, None], slot_top[:, None, :, :], NEGATIVE), axis=2
    )
    weights = jnp.where(live_mask, jnp.exp(scores - request_top[:, owners][..., None]), 0.0)
    slot_total = jnp.sum(weights, axis=3)
    slot_acc = jnp.einsum(
        "tshk,skhd->tshd",
        weights.astype(jnp.bfloat16),
        values_here,
        preferred_element_type=jnp.float32,
    )
    indicator = belongs.astype(jnp.float32)
    totals = jnp.einsum("rs,tsh->trh", indicator, slot_total, precision=lax.Precision.HIGHEST)
    accums = jnp.einsum("rs,tshd->trhd", indicator, slot_acc, precision=lax.Precision.HIGHEST)
    return (request_top, totals, accums)


def shards(
    tokens,
    norm_gains,
    w_qkv,
    w_out,
    w_gate_up,
    w_down,
    k_cache,
    v_cache,
    lengths,
    slot_request,
    slot_page,
    move_slot,
    move_offset,
):
    step_count, req_count, width_here = tokens.shape
    row_count = step_count * req_count
    activ = tokens.reshape(row_count, width_here).astype(jnp.float32)

    def finish_qkv(total, squares, rows_here):
        count = total.shape[0]
        inverse = lax.rsqrt(squares / D + EPSILON)
        scaled = total * inverse[:, None, None]
        heads_here = scaled.shape[2] // HEAD_DIM
        query_rows = rotate(scaled[:, 0].reshape(count, heads_here, HEAD_DIM), rows_here)
        key_rows = rotate(scaled[:, 1].reshape(count, heads_here, HEAD_DIM), rows_here)
        return (
            query_rows.reshape(count, -1).astype(jnp.bfloat16),
            key_rows.reshape(count, -1).astype(jnp.bfloat16),
            scaled[:, 2].astype(jnp.bfloat16),
        )

    def finish_mlp(total, squares, start):
        inverse = lax.rsqrt(squares / D + EPSILON)
        gate = total[:, 0] * inverse[:, None]
        upward = total[:, 1] * inverse[:, None]
        return ((jax.nn.silu(gate) * upward).astype(jnp.bfloat16),)

    normed_one = (activ * norm_gains[0]).astype(jnp.bfloat16)
    partial_one = jnp.einsum("bd,dcn->bcn", normed_one, w_qkv, preferred_element_type=jnp.float32)
    squares_one = jnp.sum(activ * activ, axis=1)
    sending = migrate_pool(k_cache, v_cache, move_slot, move_offset)
    holders = lax.axis_size("pages")
    myself = lax.axis_index("pages")
    group = req_count // holders
    packed = jnp.concatenate([partial_one.reshape(row_count, -1), squares_one[:, None]], axis=1)
    packed = jnp.moveaxis(packed.reshape(step_count, holders, group, -1), 1, 0)
    packed = lax.all_to_all(packed, "pages", split_axis=0, concat_axis=0, tiled=True)
    packed = jnp.sum(packed, axis=0).reshape(step_count * group, -1)
    own_lengths = lax.dynamic_slice_in_dim(lengths, myself * group, group)
    own_positions = (
        own_lengths[None, :] + jnp.arange(step_count, dtype=jnp.int32)[:, None]
    ).reshape(-1)
    query_own, key_own, value_own = finish_qkv(
        packed[:, :-1].reshape((step_count * group,) + partial_one.shape[1:]), packed[:, -1], own_positions
    )
    heads_here = query_own.shape[1] // HEAD_DIM
    query_gathered = gather_blocks(query_own.reshape(step_count, group, -1), "pages")
    query_gathered, sending = lax.optimization_barrier((query_gathered, sending))
    queries = jnp.moveaxis(query_gathered, 0, 1).reshape(step_count, req_count, heads_here, HEAD_DIM)
    queries_mine = query_own.reshape(step_count, group, heads_here, HEAD_DIM)
    key_mine = key_own.reshape(step_count, group, heads_here, HEAD_DIM)
    value_mine = value_own.reshape(step_count, group, heads_here, HEAD_DIM)
    cache_top, cache_total, cache_acc = local_attention(
        queries, k_cache, v_cache, lengths, slot_request, slot_page
    )
    holders = lax.axis_size("pages")
    myself = lax.axis_index("pages")
    group = req_count // holders
    packed = jnp.concatenate(
        [cache_acc, cache_total[..., None], cache_top[..., None]], axis=-1
    ).reshape(step_count, holders, group, heads_here, HEAD_DIM + 2)
    packed = jnp.moveaxis(packed, 1, 0)
    packed, received = lax.optimization_barrier((packed, exchange_pool(sending)))
    packed = lax.all_to_all(packed, "pages", split_axis=0, concat_axis=0, tiled=True)
    part_acc = packed[..., :HEAD_DIM]
    part_total = packed[..., HEAD_DIM]
    part_top = packed[..., HEAD_DIM + 1]
    scale = HEAD_DIM ** (-0.5)
    step_ids = jnp.arange(step_count, dtype=jnp.int32)
    causal = (step_ids[:, None] >= step_ids[None, :])[:, :, None, None]
    fresh = (
        jnp.einsum("trhd,urhd->turh", queries_mine, key_mine, preferred_element_type=jnp.float32)
        * scale
    )
    fresh = jnp.where(causal, fresh, NEGATIVE)
    row_top = jnp.maximum(jnp.max(part_top, axis=0), jnp.max(fresh, axis=1))
    carried = jnp.exp(part_top - row_top[None])
    fresh_w = jnp.where(causal, jnp.exp(fresh - row_top[:, None]), 0.0)
    totals = jnp.sum(part_total * carried, axis=0) + jnp.sum(fresh_w, axis=1)
    accums = jnp.sum(part_acc * carried[..., None], axis=0) + jnp.einsum(
        "turh,urhd->trhd",
        fresh_w.astype(jnp.bfloat16),
        value_mine,
        preferred_element_type=jnp.float32,
    )
    attended_mine = (accums / totals[..., None]).astype(jnp.bfloat16)
    attended = jnp.moveaxis(gather_blocks(attended_mine, "pages"), 0, 1).reshape(
        row_count, heads_here * HEAD_DIM
    )
    mixed = activ + across_heads(
        lax.dot_general(attended, w_out, CONTRACT_LAST, preferred_element_type=jnp.float32)
    )
    normed_two = (mixed * norm_gains[1]).astype(jnp.bfloat16)
    partial_two = jnp.einsum(
        "bd,gdf->bgf", normed_two, w_gate_up, preferred_element_type=jnp.float32
    )
    squares_two = jnp.sum(mixed * mixed, axis=1)
    (hidden,) = reduce_rows(partial_two, squares_two, finish_mlp, carrier=jnp.bfloat16)
    feed = across_heads(
        lax.dot_general(hidden, w_down, CONTRACT_LAST, preferred_element_type=jnp.float32)
    )
    layer_out = (mixed + feed).astype(jnp.bfloat16).reshape(step_count, req_count, width_here)
    new_k_cache, new_v_cache = land_pool(k_cache, v_cache, *received, move_slot, move_offset)
    return (layer_out, new_k_cache, new_v_cache)


def solution(mesh):
    in_specs = (
        P(None, None, "pages"),
        P(None, "pages"),
        P("pages", None, "mp"),
        P("pages", "mp"),
        P(None, "pages", "mp"),
        P("pages", "mp"),
        P("pages", None, "mp"),
        P("pages", None, "mp"),
        P(),
        P(),
        P(),
        P(),
        P(),
    )
    out_specs = (P(None, None, "pages"), P("pages", None, "mp"), P("pages", None, "mp"))
    return jax.shard_map(shards, mesh=mesh, in_specs=in_specs, out_specs=out_specs, check_vma=False)
```

```python
import jax
import jax.numpy as jnp
from jax import lax
from jax.sharding import PartitionSpec as P

D = 3072
HEAD_DIM = 96


EPSILON = 1e-05
NEGATIVE = -1e30
THETA = 10000.0
CONTRACT_LAST = (((1,), (1,)), ((), ()))


def merged(part, axis, combine):
    gathered = jax.tree.map(lambda a: lax.all_gather(a, axis), part)

    def take(source):
        return jax.tree.map(lambda a: lax.dynamic_index_in_dim(a, source, 0, False), gathered)

    return lax.fori_loop(
        1, lax.axis_size(axis), lambda source, state: combine(state, take(source)), take(0)
    )


def rotate(values, positions):
    half_dim = values.shape[-1] // 2
    exponent = jnp.arange(half_dim, dtype=jnp.float32) * (-2.0 / values.shape[-1])
    frequency = jnp.power(jnp.float32(THETA), exponent)
    angles = positions.astype(jnp.float32)[:, None, None] * frequency[None, None, :]
    cosine = jnp.cos(angles)
    sine = jnp.sin(angles)
    first = values[..., :half_dim]
    second = values[..., half_dim:]
    return jnp.concatenate(
        [first * cosine - second * sine, second * cosine + first * sine], axis=-1
    )


def merge_parts(first, second):
    top_a, total_a, accum_a = first
    top_b, total_b, accum_b = second
    joined = jnp.maximum(top_a, top_b)
    factor_a = jnp.exp(top_a - joined)
    factor_b = jnp.exp(top_b - joined)
    return (
        joined,
        total_a * factor_a + total_b * factor_b,
        accum_a * factor_a[..., None] + accum_b * factor_b[..., None],
    )


def reduce_rows(partial_value, squares, finish, tied=None, carrier=jnp.float32):
    rows = partial_value.shape[0]
    holders = lax.axis_size("pages")
    block = rows // holders
    packed = jnp.concatenate([partial_value.reshape(rows, -1), squares[:, None]], axis=1)
    packed = packed.reshape(holders, block, packed.shape[1]).astype(carrier)
    packed = lax.all_to_all(packed, "pages", split_axis=0, concat_axis=0, tiled=True)
    packed = jnp.sum(packed.astype(jnp.float32), axis=0)
    start = lax.axis_index("pages") * block
    done = finish(packed[:, :-1].reshape((block,) + partial_value.shape[1:]), packed[:, -1], start)
    width = [part.shape[1] for part in done]
    joined = gather_blocks(jnp.concatenate(done, axis=1), "pages").reshape(rows, sum(width))
    pieces = []
    offset = 0
    for size in width:
        pieces.append(joined[:, offset : offset + size])
        offset += size
    if tied is not None:
        return lax.optimization_barrier((tuple(pieces), tied))
    return tuple(pieces)


def gather_blocks(block, axis):
    count = lax.axis_size(axis)
    spread = jnp.broadcast_to(block[None], (count,) + block.shape)
    return lax.all_to_all(spread, axis, split_axis=0, concat_axis=0, tiled=True)


def across_heads(term):
    return jnp.sum(gather_blocks(term, "mp"), axis=0)


def migrate_pool(key_local, value_local, move_slot, move_offset):
    holders = lax.axis_size("pages")
    myself = lax.axis_index("pages")
    mine = lax.dynamic_index_in_dim(move_slot, myself, 0, keepdims=False)
    targets = (myself + move_offset) % holders
    holder_ids = jnp.arange(holders, dtype=jnp.int32)
    aimed = holder_ids[:, None] == targets[None, :]
    chosen = jnp.sum(jnp.where(aimed, mine[None, :], 0), axis=1)
    sending = jnp.any(aimed, axis=1)[:, None, None]
    key_send = jnp.where(sending, key_local[chosen], jnp.zeros((), key_local.dtype))
    value_send = jnp.where(sending, value_local[chosen], jnp.zeros((), value_local.dtype))
    return jnp.stack([key_send, value_send], axis=1)


def exchange_pool(both):
    return lax.all_to_all(both, "pages", split_axis=0, concat_axis=0, tiled=True)


def land_pool(key_local, value_local, both_recv, move_slot, move_offset):
    holders = lax.axis_size("pages")
    myself = lax.axis_index("pages")
    mine = lax.dynamic_index_in_dim(move_slot, myself, 0, keepdims=False)
    sources = (myself - move_offset) % holders
    slot_ids = jnp.arange(key_local.shape[0], dtype=jnp.int32)
    landing = slot_ids[:, None] == mine[None, :]
    came_from = jnp.sum(jnp.where(landing, sources[None, :], 0), axis=1)
    arriving = jnp.any(landing, axis=1)[:, None, None]
    picked = both_recv[came_from]
    return (
        jnp.where(arriving, picked[:, 0], key_local),
        jnp.where(arriving, picked[:, 1], value_local),
    )


def local_attention(queries, k_cache, v_cache, lengths, slot_request, slot_page):
    step_count, req_count, heads_here, head_dim = queries.shape
    slot_count, page_len, channels = k_cache.shape
    scale = head_dim ** (-0.5)
    myself = lax.axis_index("pages")
    own_request = lax.dynamic_slice_in_dim(slot_request, myself * slot_count, slot_count)
    own_page = lax.dynamic_slice_in_dim(slot_page, myself * slot_count, slot_count)
    owners = jnp.clip(own_request, 0, req_count - 1)
    key_pos = own_page[:, None] * page_len + jnp.arange(page_len, dtype=jnp.int32)[None, :]
    usable = (own_request >= 0)[:, None] & (key_pos < lengths[owners][:, None])
    keys_here = k_cache.reshape(slot_count, page_len, heads_here, head_dim)
    values_here = v_cache.reshape(slot_count, page_len, heads_here, head_dim)
    scores = (
        jnp.einsum(
            "tshd,skhd->tshk", queries[:, owners], keys_here, preferred_element_type=jnp.float32
        )
        * scale
    )
    live_mask = usable[None, :, None, :]
    scores = jnp.where(live_mask, scores, NEGATIVE)
    slot_top = jnp.max(scores, axis=3)
    belongs = own_request[None, :] == jnp.arange(req_count, dtype=jnp.int32)[:, None]
    request_top = jnp.max(
        jnp.where(belongs[None, :, :, None], slot_top[:, None, :, :], NEGATIVE), axis=2
    )
    weights = jnp.where(live_mask, jnp.exp(scores - request_top[:, owners][..., None]), 0.0)
    slot_total = jnp.sum(weights, axis=3)
    slot_acc = jnp.einsum(
        "tshk,skhd->tshd",
        weights.astype(jnp.bfloat16),
        values_here,
        preferred_element_type=jnp.float32,
    )
    indicator = belongs.astype(jnp.float32)
    totals = jnp.einsum("rs,tsh->trh", indicator, slot_total, precision=lax.Precision.HIGHEST)
    accums = jnp.einsum("rs,tshd->trhd", indicator, slot_acc, precision=lax.Precision.HIGHEST)
    return (request_top, totals, accums)


def shards(
    tokens,
    norm_gains,
    w_qkv,
    w_out,
    w_gate_up,
    w_down,
    k_cache,
    v_cache,
    lengths,
    slot_request,
    slot_page,
    move_slot,
    move_offset,
):
    step_count, req_count, width_here = tokens.shape
    row_count = step_count * req_count
    activ = tokens.reshape(row_count, width_here).astype(jnp.float32)

    def finish_qkv(total, squares, rows_here):
        count = total.shape[0]
        inverse = lax.rsqrt(squares / D + EPSILON)
        scaled = total * inverse[:, None, None]
        heads_here = scaled.shape[2] // HEAD_DIM
        query_rows = rotate(scaled[:, 0].reshape(count, heads_here, HEAD_DIM), rows_here)
        key_rows = rotate(scaled[:, 1].reshape(count, heads_here, HEAD_DIM), rows_here)
        return (
            query_rows.reshape(count, -1).astype(jnp.bfloat16),
            key_rows.reshape(count, -1).astype(jnp.bfloat16),
            scaled[:, 2].astype(jnp.bfloat16),
        )

    def finish_mlp(total, squares, start):
        inverse = lax.rsqrt(squares / D + EPSILON)
        gate = total[:, 0] * inverse[:, None]
        upward = total[:, 1] * inverse[:, None]
        return ((jax.nn.silu(gate) * upward).astype(jnp.bfloat16),)

    normed_one = (activ * norm_gains[0]).astype(jnp.bfloat16)
    partial_one = jnp.einsum("bd,dcn->bcn", normed_one, w_qkv, preferred_element_type=jnp.float32)
    squares_one = jnp.sum(activ * activ, axis=1)
    sending = migrate_pool(k_cache, v_cache, move_slot, move_offset)
    holders = lax.axis_size("pages")
    myself = lax.axis_index("pages")
    group = req_count // holders
    packed = jnp.concatenate([partial_one.reshape(row_count, -1), squares_one[:, None]], axis=1)
    packed = jnp.moveaxis(packed.reshape(step_count, holders, group, -1), 1, 0)
    packed = lax.all_to_all(packed, "pages", split_axis=0, concat_axis=0, tiled=True)
    packed = jnp.sum(packed, axis=0).reshape(step_count * group, -1)
    own_lengths = lax.dynamic_slice_in_dim(lengths, myself * group, group)
    own_positions = (
        own_lengths[None, :] + jnp.arange(step_count, dtype=jnp.int32)[:, None]
    ).reshape(-1)
    query_own, key_own, value_own = finish_qkv(
        packed[:, :-1].reshape((step_count * group,) + partial_one.shape[1:]), packed[:, -1], own_positions
    )
    heads_here = query_own.shape[1] // HEAD_DIM
    query_gathered = gather_blocks(query_own.reshape(step_count, group, -1), "pages")
    query_gathered, sending = lax.optimization_barrier((query_gathered, sending))
    queries = jnp.moveaxis(query_gathered, 0, 1).reshape(step_count, req_count, heads_here, HEAD_DIM)
    queries_mine = query_own.reshape(step_count, group, heads_here, HEAD_DIM)
    key_mine = key_own.reshape(step_count, group, heads_here, HEAD_DIM)
    value_mine = value_own.reshape(step_count, group, heads_here, HEAD_DIM)
    cache_top, cache_total, cache_acc = local_attention(
        queries, k_cache, v_cache, lengths, slot_request, slot_page
    )
    holders = lax.axis_size("pages")
    myself = lax.axis_index("pages")
    group = req_count // holders
    packed = jnp.concatenate(
        [cache_acc, cache_total[..., None], cache_top[..., None]], axis=-1
    ).reshape(step_count, holders, group, heads_here, HEAD_DIM + 2)
    packed = jnp.moveaxis(packed, 1, 0)
    packed, received = lax.optimization_barrier((packed, exchange_pool(sending)))
    packed = lax.all_to_all(packed, "pages", split_axis=0, concat_axis=0, tiled=True)
    part_acc = packed[..., :HEAD_DIM]
    part_total = packed[..., HEAD_DIM]
    part_top = packed[..., HEAD_DIM + 1]
    scale = HEAD_DIM ** (-0.5)
    step_ids = jnp.arange(step_count, dtype=jnp.int32)
    causal = (step_ids[:, None] >= step_ids[None, :])[:, :, None, None]
    fresh = (
        jnp.einsum("trhd,urhd->turh", queries_mine, key_mine, preferred_element_type=jnp.float32)
        * scale
    )
    fresh = jnp.where(causal, fresh, NEGATIVE)
    row_top = jnp.maximum(jnp.max(part_top, axis=0), jnp.max(fresh, axis=1))
    carried = jnp.exp(part_top - row_top[None])
    fresh_w = jnp.where(causal, jnp.exp(fresh - row_top[:, None]), 0.0)
    totals = jnp.sum(part_total * carried, axis=0) + jnp.sum(fresh_w, axis=1)
    accums = jnp.sum(part_acc * carried[..., None], axis=0) + jnp.einsum(
        "turh,urhd->trhd",
        fresh_w.astype(jnp.bfloat16),
        value_mine,
        preferred_element_type=jnp.float32,
    )
    attended_mine = (accums / totals[..., None]).astype(jnp.bfloat16)
    attended = jnp.moveaxis(gather_blocks(attended_mine, "pages"), 0, 1).reshape(
        row_count, heads_here * HEAD_DIM
    )
    mixed = activ + across_heads(
        lax.dot_general(attended, w_out, CONTRACT_LAST, preferred_element_type=jnp.float32)
    )
    normed_two = (mixed * norm_gains[1]).astype(jnp.bfloat16)
    partial_two = jnp.einsum(
        "bd,gdf->bgf", normed_two, w_gate_up, preferred_element_type=jnp.float32
    )
    squares_two = jnp.sum(mixed * mixed, axis=1)
    (hidden,) = reduce_rows(partial_two, squares_two, finish_mlp, carrier=jnp.bfloat16)
    feed = across_heads(
        lax.dot_general(hidden, w_down, CONTRACT_LAST, preferred_element_type=jnp.float32)
    )
    layer_out = (mixed + feed).astype(jnp.bfloat16).reshape(step_count, req_count, width_here)
    new_k_cache, new_v_cache = land_pool(k_cache, v_cache, received, move_slot, move_offset)
    return (layer_out, new_k_cache, new_v_cache)


def solution(mesh):
    in_specs = (
        P(None, None, "pages"),
        P(None, "pages"),
        P("pages", None, "mp"),
        P("pages", "mp"),
        P(None, "pages", "mp"),
        P("pages", "mp"),
        P("pages", None, "mp"),
        P("pages", None, "mp"),
        P(),
        P(),
        P(),
        P(),
        P(),
    )
    out_specs = (P(None, None, "pages"), P("pages", None, "mp"), P("pages", None, "mp"))
    return jax.shard_map(shards, mesh=mesh, in_specs=in_specs, out_specs=out_specs, check_vma=False)
```
